512 devices in a mesh: wide: 128 (over y, z, core), narrow: 4 (over x).
Axes of the slice: x: 4, y: 4, z: 16, core: 2. Of those that a mesh axis runs over, the one named last changes fastest.
Arguments:
- rhs: float32 [512, 65536], P(None, ('wide', 'narrow')), may hold values from -20 to 20
- levels: int32 [65536], P(('wide', 'narrow')), may hold values from 0 to 3
- face_source: int32 [6, 65536], P(None, ('wide', 'narrow')), may hold values from -1 to 1343, as said below
- subface: int32 [6, 65536], P(None, ('wide', 'narrow')), may hold values from 0 to 4
- orientation: int32 [6, 65536], P(None, ('wide', 'narrow')), may hold values from 0 to 7
- send_list: int32 [512, 576], P(('wide', 'narrow')), may hold values from 0 to 767
- parent: int32 [128, 512], P('wide', 'narrow'), may hold values from 0 to 127, never falling along the last dimension, each value on 1 to 8 neighbouring positions
- coarse_inverse: float32 [128, 128, 128], P('wide'), may hold values from -1.5 to 1.5, as said below
Outputs:
- corrected: float32 [512, 65536], P(None, ('wide', 'narrow'))
- residual: float32 [512, 65536], P(None, ('wide', 'narrow'))
The draws below stay inside these ranges and needn't reach their ends.
Inputs may be any that keep to these rules, and one draw needn't show every extreme that they name: `face_source`: exactly 288 faces of each device name a source device and slot, no slot twice; sources lie in the device's own block or in the blocks just before and after it along wide, never outside the mesh; every device names all 48 slots of some device of its own block; -1 marks a boundary face. `coarse_inverse`: diagonal entries lie in 0.5 to 1.5.
All inputs are finite; a program needn't handle non-finite values.
Results may differ from the reference program's by a relative error of at most 0.00023.
Values sent between devices are 32-bit elements; how exact they have to be, the bound alone decides.
No kernel may reach another device: no remote copies, remote signals or barrier semaphores. Data moves between devices by JAX's collectives and lax.ppermute only.
A program may use at most 64 MiB of HBM per device.

```python
import math
import jax
import jax.numpy as jnp
import numpy as np
from jax import lax

NODES = 8
E_DEV = 128
CAP = 48
POWER = 3
CHEB = 4
DEVS = 512
ELEMS = 65536
CB = 128
N_WIDE = 128
N_NARROW = 4


def draw_rhs(key, part):
    keys = jax.random.split(key, 3)
    values = NODES * NODES * NODES
    position = jnp.arange(ELEMS).astype(jnp.float32) / ELEMS
    rising = 1.0 + 2.0 * position
    roughness = jax.random.uniform(keys[0], (ELEMS,), jnp.float32, 0.1, 1.0)
    noise = jax.random.normal(keys[1], (values, ELEMS), jnp.float32)
    smooth = jax.random.normal(keys[2], (ELEMS,), jnp.float32)
    result = rising[None, :] * (roughness[None, :] * noise + (1.0 - roughness[None, :]) * smooth[None, :])
    return jnp.clip(result, -20.0, 20.0).astype(jnp.float32)


def draw_face_source(key, part):
    faces = 6 * E_DEV
    slots = 3 * N_NARROW * CAP
    remote_count = 6 * CAP
    offset = jax.random.randint(jax.random.fold_in(key, 7), (), 0, 3)

    def one_device(index):
        device_key = jax.random.fold_in(key, index + 11)
        keys = jax.random.split(device_key, 4)
        wide_pos = index // N_NARROW
        narrow_pos = index % N_NARROW
        places = jax.random.permutation(keys[0], faces)
        scores = jax.random.permutation(keys[1], slots)
        slot_ids = jnp.arange(slots)
        groups = slot_ids // (N_NARROW * CAP)
        owners = slot_ids // CAP % N_NARROW
        source_wide = wide_pos + groups - 1
        usable = (source_wide >= 0) & (source_wide < N_WIDE)
        forced_peer = (narrow_pos + 1 + offset) % N_NARROW
        forced = (groups == 1) & (owners == forced_peer)
        scores = jnp.where(forced, scores - slots, scores)
        scores = jnp.where((slot_ids == slots - 1) & usable, scores - 2 * slots, scores)
        scores = jnp.where(usable, scores, scores + 4 * slots)
        chosen = jnp.argsort(scores, stable=True)[:remote_count]
        local_pick = jax.random.randint(keys[2], (faces,), 0, faces)
        border = jax.random.randint(keys[3], (faces,), 0, 8) == 0
        values = jnp.where(border, -1, local_pick)
        values = values.at[places[:remote_count]].set(faces + chosen)
        return values.reshape(6, E_DEV)
    stacked = jax.vmap(one_device)(jnp.arange(DEVS))
    return jnp.transpose(stacked, (1, 0, 2)).reshape(6, ELEMS).astype(jnp.int32)


def draw_coarse_inverse(key, part):
    keys = jax.random.split(key, 2)
    identity = jnp.arange(CB)[:, None] == jnp.arange(CB)[None, :]
    diagonal = jax.random.uniform(keys[0], (N_WIDE, CB, CB), jnp.float32, 0.5, 1.5)
    spread = 1.0 / jnp.sqrt(jnp.float32(CB))
    offdiag = jnp.clip(0.5 * jax.random.normal(keys[1], (N_WIDE, CB, CB), jnp.float32), -2.5, 2.5) * spread
    return jnp.where(identity[None, :, :], diagonal, offdiag).astype(jnp.float32)


def plant(values, own_key, least, high):
    spot = [jax.random.randint(jax.random.fold_in(own_key, axis), (), 0, length) for axis, length in enumerate(values.shape)]
    widest = values.shape.index(max(values.shape))
    next_to = spot[:widest] + [(spot[widest] + 1) % values.shape[widest]] + spot[widest + 1:]
    return values.at[tuple(spot)].set(least).at[tuple(next_to)].set(high)


def profile(count, total, reach, slope):
    portions = [(1 << 20) // math.isqrt(standing ** slope) + 1 for standing in range(2, count + 1)]
    surplus, counts = total - reach - (count - 1), [1] * (count - 1)
    while surplus > 0:
        candidates = [i for i in range(count - 1) if counts[i] < reach]
        whole, remaining = sum([portions[i] for i in candidates]), surplus
        for i in candidates:
            addition = min(reach - counts[i], max(1, remaining * portions[i] // whole), surplus)
            counts[i] = counts[i] + addition
            surplus = surplus - addition
    return np.array([reach] + counts)


def ragged_sizes(stream_key, amount, total, reach, skew):
    if amount == 2:
        one = jax.random.randint(stream_key, (), max(1, total - reach), min(reach, total - 1) + 1)
        return jnp.stack([one, total - one])
    tallies = jnp.asarray(profile(amount, total, reach, skew), jnp.int32)
    pairs = (amount - 1) // 2
    giver, sink = tallies[1:1 + 2 * pairs:2], tallies[2:2 + 2 * pairs:2]
    margin = jnp.minimum(giver - 1, reach - sink)
    moved = jax.random.randint(jax.random.fold_in(stream_key, 1), (pairs,), 0, 1 << 20) % (margin + 1)
    tallies = tallies.at[1:1 + 2 * pairs:2].set(giver - moved).at[2:2 + 2 * pairs:2].set(sink + moved)
    return tallies[jax.random.permutation(jax.random.fold_in(stream_key, 2), amount)]


def setup_inputs(seed: int = 0) -> dict:
    arg_keys = jax.random.split(jax.random.key(seed), 9)
    rhs = draw_rhs(jax.random.fold_in(arg_keys[8], 71), 0)
    levels = plant(jax.random.randint(arg_keys[1], (ELEMS,), 0, 4), jax.random.fold_in(arg_keys[1], 1), 0, 3).astype(jnp.int32)
    face_source = draw_face_source(jax.random.fold_in(arg_keys[8], 71), 0)
    subface = plant(jax.random.randint(arg_keys[3], (6, ELEMS), 0, 5), jax.random.fold_in(arg_keys[3], 1), 0, 4).astype(jnp.int32)
    orientation = plant(jax.random.randint(arg_keys[4], (6, ELEMS), 0, 8), jax.random.fold_in(arg_keys[4], 1), 0, 7).astype(jnp.int32)
    send_list = plant(jax.random.randint(arg_keys[5], (DEVS, 3 * N_NARROW * CAP), 0, 6 * E_DEV), jax.random.fold_in(arg_keys[5], 1), 0, (6 * E_DEV) - 1).astype(jnp.int32)
    parent = jax.vmap(lambda own: jnp.searchsorted(jnp.cumsum(ragged_sizes(own, CB, N_NARROW * E_DEV, 8, 0)), jnp.arange(N_NARROW * E_DEV), side="right"))(jax.random.split(arg_keys[6], N_WIDE)).reshape((N_WIDE, N_NARROW * E_DEV)).astype(jnp.int32)
    coarse_inverse = draw_coarse_inverse(jax.random.fold_in(arg_keys[8], 71), 0)
    return {"rhs": rhs, "levels": levels, "face_source": face_source, "subface": subface, "orientation": orientation, "send_list": send_list, "parent": parent, "coarse_inverse": coarse_inverse}


PENALTY = 32.0
SAFETY = 1.2
RANGE_RATIO = 8.0
HIGHEST = lax.Precision.HIGHEST

def legendre_rows(points, count):
    rows_list = [points * 0.0 + 1.0, points.copy()]
    for order in range(2, count):
        rows_list.append(((2 * order - 1) * points * rows_list[order - 1] - (order - 1) * rows_list[order - 2]) / order)
    return rows_list

def gll_tables(count):
    degree_top = count - 1
    node_pos = np.cos(np.pi * np.arange(count) / degree_top)
    for newton_step in range(60):
        values_table = legendre_rows(node_pos, count)
        node_pos = node_pos - (node_pos * values_table[degree_top] - values_table[degree_top - 1]) / (count * values_table[degree_top])
    node_pos = node_pos[::-1].copy()
    node_pos[0] = -1.0
    node_pos[-1] = 1.0
    values_table = legendre_rows(node_pos, count)
    weights = 2.0 / (degree_top * count * values_table[degree_top] ** 2)
    barycentric = np.array([1.0 / np.prod([node_pos[j] - node_pos[k] for k in range(count) if k != j]) for j in range(count)])
    derivative = np.zeros((count, count))
    for i in range(count):
        for j in range(count):
            if i != j:
                derivative[i, j] = barycentric[j] / barycentric[i] / (node_pos[i] - node_pos[j])
        derivative[i, i] = -np.sum(derivative[i])
    stiffness = derivative.T @ (weights[:, None] * derivative)

    def interpolate(targets):
        matrix = np.ones((count, count))
        for j in range(count):
            for k in range(count):
                if k != j:
                    matrix[:, j] *= (targets - node_pos[k]) / (node_pos[j] - node_pos[k])
        return matrix
    half_low = interpolate((node_pos - 1.0) / 2.0)
    half_high = interpolate((node_pos + 1.0) / 2.0)
    return tuple((jnp.asarray(table, dtype=jnp.float32) for table in (weights, stiffness, half_low, half_high)))

def face_traces(cube):
    return jnp.stack([cube[0], cube[-1], cube[:, 0], cube[:, -1], cube[:, :, 0], cube[:, :, -1]])

def add_faces(cube, values):
    cube = cube.at[0].add(values[0]).at[-1].add(values[1])
    cube = cube.at[:, 0].add(values[2]).at[:, -1].add(values[3])
    return cube.at[:, :, 0].add(values[4]).at[:, :, -1].add(values[5])

def orient_faces(neighbour, orientation, subface, half_low, half_high):
    bit_one = (orientation % 2)[:, None, None, :] == 1
    bit_two = (orientation // 2 % 2)[:, None, None, :] == 1
    bit_four = (orientation // 4)[:, None, None, :] == 1
    turned = jnp.where(bit_one, neighbour[:, ::-1], neighbour)
    turned = jnp.where(bit_two, turned[:, :, ::-1], turned)
    turned = jnp.where(bit_four, jnp.swapaxes(turned, 1, 2), turned)
    hanging = (subface > 0)[:, None, None, :]
    quad_first = ((subface - 1) % 2)[:, None, None, :] == 0
    quad_second = ((subface - 1) // 2)[:, None, None, :] == 0
    low_first = jnp.einsum('ai,fibe->fabe', half_low, turned, precision=HIGHEST)
    high_first = jnp.einsum('ai,fibe->fabe', half_high, turned, precision=HIGHEST)
    first_pass = jnp.where(quad_first, low_first, high_first)
    low_second = jnp.einsum('bj,faje->fabe', half_low, first_pass, precision=HIGHEST)
    high_second = jnp.einsum('bj,faje->fabe', half_high, first_pass, precision=HIGHEST)
    second_pass = jnp.where(quad_second, low_second, high_second)
    return jnp.where(hanging, second_pass, turned)

def cell_term(cube, weights, stiffness):
    first_axis = jnp.einsum('ai,ijke->ajke', stiffness, cube, precision=HIGHEST) * (weights[None, :, None, None] * weights[None, None, :, None])
    second_axis = jnp.einsum('bj,ijke->ibke', stiffness, cube, precision=HIGHEST) * (weights[:, None, None, None] * weights[None, None, :, None])
    third_axis = jnp.einsum('ck,ijke->ijce', stiffness, cube, precision=HIGHEST) * (weights[:, None, None, None] * weights[None, :, None, None])
    return first_axis + second_axis + third_axis

def apply_operator(field, fetch, scale, orientation, subface, tables):
    weights, stiffness, half_low, half_high = tables
    count = weights.shape[0]
    cube = field.reshape(count, count, count, -1)
    traces = face_traces(cube)
    neighbour = orient_faces(fetch(traces), orientation, subface, half_low, half_high)
    face_mass = weights[:, None] * weights[None, :]
    jumps = PENALTY * face_mass[None, :, :, None] * (traces - neighbour)
    total = add_faces(cell_term(cube, weights, stiffness), jumps)
    return total.reshape(count * count * count, -1) * scale[None, :]

def diag_pattern(tables):
    weights, stiffness, half_low, half_high = tables
    count = weights.shape[0]
    stiff_diag = jnp.diagonal(stiffness)
    cell_diag = stiff_diag[:, None, None] * weights[None, :, None] * weights[None, None, :] + weights[:, None, None] * stiff_diag[None, :, None] * weights[None, None, :] + weights[:, None, None] * weights[None, :, None] * stiff_diag[None, None, :]
    face_mass = PENALTY * weights[:, None] * weights[None, :]
    face_values = jnp.broadcast_to(face_mass[None, :, :, None], (6, count, count, 1))
    pattern = add_faces(cell_diag[:, :, :, None], face_values)
    return pattern.reshape(count * count * count)

def reference(rhs, levels, face_source, subface, orientation, send_list, parent, coarse_inverse):
    tables = gll_tables(NODES)
    weights = tables[0]
    count = NODES
    elem_count = rhs.shape[1]
    scale = jnp.exp2(-levels.astype(jnp.float32))
    inv_diag = 1.0 / (diag_pattern(tables)[:, None] * scale[None, :])
    owner_dev = (jnp.arange(elem_count) // E_DEV).astype(jnp.int32)
    own_wide = (owner_dev // N_NARROW).astype(jnp.int32)
    own_narrow = (owner_dev % N_NARROW).astype(jnp.int32)
    remote = face_source - 6 * E_DEV
    group = jnp.clip(remote // (N_NARROW * CAP), 0, 2)
    peer = remote // CAP % N_NARROW
    slot = remote % CAP
    src_wide = own_wide[None, :] + group - 1
    valid = (src_wide >= 0) & (src_wide < N_WIDE)
    sender = (jnp.clip(src_wide, 0, N_WIDE - 1) * N_NARROW + peer).astype(jnp.int32)
    slot_pos = (((2 - group) * N_NARROW + own_narrow[None, :]) * CAP + slot).astype(jnp.int32)
    sent = send_list[sender, slot_pos]
    columns = jnp.where(face_source < 0, 6 * elem_count, jnp.where(face_source < 6 * E_DEV, owner_dev[None, :] * 6 * E_DEV + face_source, jnp.where(valid, sender * 6 * E_DEV + sent, 6 * elem_count))).astype(jnp.int32)
    devices = N_WIDE * N_NARROW

    def fetch(traces):
        pool = traces.reshape(6, count * count, devices, E_DEV).transpose(1, 2, 0, 3).reshape(count * count, 6 * elem_count)
        pool = jnp.concatenate([pool, jnp.zeros((count * count, 1), jnp.float32)], axis=1)
        picked = pool[:, columns.reshape(-1)]
        return picked.reshape(count * count, 6, elem_count).transpose(1, 0, 2).reshape(6, count, count, elem_count)

    def operator(field):
        return apply_operator(field, fetch, scale, orientation, subface, tables)
    vector = rhs
    previous = rhs
    for iteration in range(POWER):
        previous = vector
        vector = inv_diag * operator(vector)
    estimate = jnp.sqrt(jnp.sum(vector * vector) / jnp.sum(previous * previous))
    lam_max = SAFETY * estimate
    lam_min = lam_max / RANGE_RATIO
    theta = (lam_max + lam_min) / 2.0
    delta = (lam_max - lam_min) / 2.0
    sigma = theta / delta
    rho_now = 1.0 / sigma
    direction = inv_diag * rhs / theta
    solution = direction
    for iteration in range(CHEB - 1):
        resid = rhs - operator(solution)
        rho_new = 1.0 / (2.0 * sigma - rho_now)
        direction = rho_new * rho_now * direction + 2.0 * rho_new / delta * inv_diag * resid
        solution = solution + direction
        rho_now = rho_new
    residual = rhs - operator(solution)
    mass = (weights[:, None, None] * weights[None, :, None] * weights[None, None, :]).reshape(count * count * count, 1)
    element_mass = lax.optimization_barrier(jnp.sum(mass * residual, axis=0)) / 8.0
    block_mass = element_mass.reshape(N_WIDE, N_NARROW * E_DEV)
    cells = coarse_inverse.shape[1]
    coarse_res = jax.vmap(lambda vals, ids: jax.ops.segment_sum(vals, ids, num_segments=cells))(block_mass, parent)
    coarse_cor = jnp.einsum('wij,wj->wi', coarse_inverse, coarse_res, precision=HIGHEST)
    correction = jnp.take_along_axis(coarse_cor, parent, axis=1).reshape(elem_count)
    corrected = solution + correction[None, :]
    return (corrected, residual)
```

```python
import jax
import jax.numpy as jnp
import numpy as np
from jax import lax
from jax.sharding import PartitionSpec as P

NODES = 8
POWER = 3
CHEB = 4


PENALTY = 32.0
SAFETY = 1.2
RANGE_RATIO = 8.0
HIGHEST = lax.Precision.HIGHEST


def legendre_rows(points, count):
    rows_list = [points * 0.0 + 1.0, points.copy()]
    for order in range(2, count):
        rows_list.append(
            ((2 * order - 1) * points * rows_list[order - 1] - (order - 1) * rows_list[order - 2])
            / order
        )
    return rows_list


def gll_tables(count):
    degree_top = count - 1
    node_pos = np.cos(np.pi * np.arange(count) / degree_top)
    for newton_step in range(60):
        values_table = legendre_rows(node_pos, count)
        node_pos = node_pos - (
            node_pos * values_table[degree_top] - values_table[degree_top - 1]
        ) / (count * values_table[degree_top])
    node_pos = node_pos[::-1].copy()
    node_pos[0] = -1.0
    node_pos[-1] = 1.0
    values_table = legendre_rows(node_pos, count)
    weights = 2.0 / (degree_top * count * values_table[degree_top] ** 2)
    barycentric = np.array(
        [
            1.0 / np.prod([node_pos[j] - node_pos[k] for k in range(count) if k != j])
            for j in range(count)
        ]
    )
    derivative = np.zeros((count, count))
    for i in range(count):
        for j in range(count):
            if i != j:
                derivative[i, j] = barycentric[j] / barycentric[i] / (node_pos[i] - node_pos[j])
        derivative[i, i] = -np.sum(derivative[i])
    stiffness = derivative.T @ (weights[:, None] * derivative)

    def interpolate(targets):
        matrix = np.ones((count, count))
        for j in range(count):
            for k in range(count):
                if k != j:
                    matrix[:, j] *= (targets - node_pos[k]) / (node_pos[j] - node_pos[k])
        return matrix

    half_low = interpolate((node_pos - 1.0) / 2.0)
    half_high = interpolate((node_pos + 1.0) / 2.0)
    return tuple(
        (
            jnp.asarray(table, dtype=jnp.float32)
            for table in (weights, stiffness, half_low, half_high)
        )
    )


def face_traces(cube):
    return jnp.stack([cube[0], cube[-1], cube[:, 0], cube[:, -1], cube[:, :, 0], cube[:, :, -1]])


def add_faces(cube, values):
    cube = cube.at[0].add(values[0]).at[-1].add(values[1])
    cube = cube.at[:, 0].add(values[2]).at[:, -1].add(values[3])
    return cube.at[:, :, 0].add(values[4]).at[:, :, -1].add(values[5])


def orient_faces(neighbour, orientation, subface, half_low, half_high):
    bit_one = (orientation % 2)[:, None, None, :] == 1
    bit_two = (orientation // 2 % 2)[:, None, None, :] == 1
    bit_four = (orientation // 4)[:, None, None, :] == 1
    turned = jnp.where(bit_one, neighbour[:, ::-1], neighbour)
    turned = jnp.where(bit_two, turned[:, :, ::-1], turned)
    turned = jnp.where(bit_four, jnp.swapaxes(turned, 1, 2), turned)
    hanging = (subface > 0)[:, None, None, :]
    quad_first = ((subface - 1) % 2)[:, None, None, :] == 0
    quad_second = ((subface - 1) // 2)[:, None, None, :] == 0
    low_first = jnp.einsum("ai,fibe->fabe", half_low, turned, precision=HIGHEST)
    high_first = jnp.einsum("ai,fibe->fabe", half_high, turned, precision=HIGHEST)
    first_pass = jnp.where(quad_first, low_first, high_first)
    low_second = jnp.einsum("bj,faje->fabe", half_low, first_pass, precision=HIGHEST)
    high_second = jnp.einsum("bj,faje->fabe", half_high, first_pass, precision=HIGHEST)
    second_pass = jnp.where(quad_second, low_second, high_second)
    return jnp.where(hanging, second_pass, turned)


def cell_term(cube, weights, stiffness):
    first_axis = jnp.einsum("ai,ijke->ajke", stiffness, cube, precision=HIGHEST) * (
        weights[None, :, None, None] * weights[None, None, :, None]
    )
    second_axis = jnp.einsum("bj,ijke->ibke", stiffness, cube, precision=HIGHEST) * (
        weights[:, None, None, None] * weights[None, None, :, None]
    )
    third_axis = jnp.einsum("ck,ijke->ijce", stiffness, cube, precision=HIGHEST) * (
        weights[:, None, None, None] * weights[None, :, None, None]
    )
    return first_axis + second_axis + third_axis


def diag_pattern(tables):
    weights, stiffness, half_low, half_high = tables
    count = weights.shape[0]
    stiff_diag = jnp.diagonal(stiffness)
    cell_diag = (
        stiff_diag[:, None, None] * weights[None, :, None] * weights[None, None, :]
        + weights[:, None, None] * stiff_diag[None, :, None] * weights[None, None, :]
        + weights[:, None, None] * weights[None, :, None] * stiff_diag[None, None, :]
    )
    face_mass = PENALTY * weights[:, None] * weights[None, :]
    face_values = jnp.broadcast_to(face_mass[None, :, :, None], (6, count, count, 1))
    pattern = add_faces(cell_diag[:, :, :, None], face_values)
    return pattern.reshape(count * count * count)


def neighbour_traces(traces, face_source, send_list):
    count = traces.shape[1]
    elements = traces.shape[3]
    wide = lax.axis_size("wide")
    local = (
        traces.reshape(6, count * count, elements)
        .transpose(1, 0, 2)
        .reshape(count * count, 6 * elements)
    )
    picked = local[:, send_list[0]]
    outgoing = picked.T.reshape(3, lax.axis_size("narrow"), -1)
    swapped = lax.all_to_all(outgoing, "narrow", split_axis=1, concat_axis=1, tiled=True)
    up = [(i, i + 1) for i in range(wide - 1)]
    down = [(i + 1, i) for i in range(wide - 1)]
    before = lax.ppermute(swapped[2], "wide", up)
    after = lax.ppermute(swapped[0], "wide", down)
    incoming = jnp.stack([before, swapped[1], after])
    received = incoming.reshape(-1, count * count).T
    pool = jnp.concatenate([local, received, jnp.zeros((count * count, 1), jnp.float32)], axis=1)
    columns = jnp.where(face_source < 0, pool.shape[1] - 1, face_source).reshape(-1)
    gathered = pool[:, columns]
    return (
        gathered.reshape(count * count, 6, elements)
        .transpose(1, 0, 2)
        .reshape(6, count, count, elements)
    )


def butterfly_sum(value):
    for axis in ("narrow", "wide"):
        size = lax.axis_size(axis)
        step = 1
        while step < size:
            pairs = [(i, i ^ step) for i in range(size)]
            value = value + lax.ppermute(value, axis, pairs)
            step *= 2
    return value


def chebyshev_coefficients(estimate):
    lam_max = SAFETY * estimate
    lam_min = lam_max / RANGE_RATIO
    theta = (lam_max + lam_min) / 2.0
    delta = (lam_max - lam_min) / 2.0
    sigma = theta / delta
    rho_now = 1.0 / sigma
    zero = jnp.zeros_like(estimate)
    direction = [1.0 / theta] + [zero] * (CHEB - 1)
    solution = list(direction)
    for iteration in range(CHEB - 1):
        scaled_resid = [1.0 - zero] + [-c for c in solution[:-1]]
        rho_new = 1.0 / (2.0 * sigma - rho_now)
        direction = [
            rho_new * rho_now * d + 2.0 * rho_new / delta * r
            for d, r in zip(direction, scaled_resid)
        ]
        solution = [s + d for s, d in zip(solution, direction)]
        rho_now = rho_new
    return solution


def body(rhs, levels, face_source, subface, orientation, send_list, parent, coarse_inverse):
    tables = gll_tables(NODES)
    weights, stiffness, half_low, half_high = tables
    count = NODES
    scale = jnp.exp2(-levels.astype(jnp.float32))
    inv_diag = 1.0 / (diag_pattern(tables)[:, None] * scale[None, :])
    face_mass = weights[:, None] * weights[None, :]

    def operator(field):
        cube = field.reshape(count, count, count, -1)
        traces = face_traces(cube)
        neighbour = orient_faces(
            neighbour_traces(traces, face_source, send_list),
            orientation,
            subface,
            half_low,
            half_high,
        )
        jumps = PENALTY * face_mass[None, :, :, None] * (traces - neighbour)
        total = add_faces(cell_term(cube, weights, stiffness), jumps)
        return total.reshape(count * count * count, -1) * scale[None, :]

    paired = jax.vmap(operator)
    power = rhs
    krylov = [inv_diag * rhs]
    images = []
    for iteration in range(POWER):
        previous = power
        both = paired(jnp.stack([power, krylov[-1]]))
        power = inv_diag * both[0]
        images.append(both[1])
        krylov.append(inv_diag * both[1])
    norms = butterfly_sum(jnp.stack([jnp.sum(power * power), jnp.sum(previous * previous)]))
    images.append(operator(krylov[-1]))

    mass = (weights[:, None, None] * weights[None, :, None] * weights[None, None, :]).reshape(
        count * count * count, 1
    )
    cells = coarse_inverse.shape[1]
    restricted = [
        jax.ops.segment_sum(jnp.sum(mass * v, axis=0) / 8.0, parent[0], num_segments=cells)
        for v in [rhs] + images
    ]
    restricted = lax.psum(jnp.stack(restricted), "narrow")

    estimate = jnp.sqrt(norms[0] / norms[1])
    coefficients = chebyshev_coefficients(estimate)
    solution = coefficients[0] * krylov[0]
    applied = coefficients[0] * images[0]
    coarse_res = restricted[0] - coefficients[0] * restricted[1]
    for j in range(1, CHEB):
        solution = solution + coefficients[j] * krylov[j]
        applied = applied + coefficients[j] * images[j]
        coarse_res = coarse_res - coefficients[j] * restricted[j + 1]
    residual = rhs - applied
    coarse_cor = jnp.dot(coarse_inverse[0], coarse_res, precision=HIGHEST)
    corrected = solution + coarse_cor[parent[0]][None, :]
    return (corrected, residual)


def solution(mesh):
    in_specs = (
        P(None, ("wide", "narrow")),
        P(("wide", "narrow")),
        P(None, ("wide", "narrow")),
        P(None, ("wide", "narrow")),
        P(None, ("wide", "narrow")),
        P(("wide", "narrow"), None),
        P("wide", "narrow"),
        P("wide", None, None),
    )
    out_specs = (P(None, ("wide", "narrow")), P(None, ("wide", "narrow")))
    return jax.shard_map(body, mesh=mesh, in_specs=in_specs, out_specs=out_specs, check_vma=False)
```

```python
import jax
import jax.numpy as jnp
import numpy as np
from jax import lax
from jax.sharding import PartitionSpec as P

NODES = 8
POWER = 3
CHEB = 4


PENALTY = 32.0
SAFETY = 1.2
RANGE_RATIO = 8.0
HIGHEST = lax.Precision.HIGHEST


def legendre_rows(points, count):
    rows_list = [points * 0.0 + 1.0, points.copy()]
    for order in range(2, count):
        rows_list.append(
            ((2 * order - 1) * points * rows_list[order - 1] - (order - 1) * rows_list[order - 2])
            / order
        )
    return rows_list


def gll_tables(count):
    degree_top = count - 1
    node_pos = np.cos(np.pi * np.arange(count) / degree_top)
    for newton_step in range(60):
        values_table = legendre_rows(node_pos, count)
        node_pos = node_pos - (
            node_pos * values_table[degree_top] - values_table[degree_top - 1]
        ) / (count * values_table[degree_top])
    node_pos = node_pos[::-1].copy()
    node_pos[0] = -1.0
    node_pos[-1] = 1.0
    values_table = legendre_rows(node_pos, count)
    weights = 2.0 / (degree_top * count * values_table[degree_top] ** 2)
    barycentric = np.array(
        [
            1.0 / np.prod([node_pos[j] - node_pos[k] for k in range(count) if k != j])
            for j in range(count)
        ]
    )
    derivative = np.zeros((count, count))
    for i in range(count):
        for j in range(count):
            if i != j:
                derivative[i, j] = barycentric[j] / barycentric[i] / (node_pos[i] - node_pos[j])
        derivative[i, i] = -np.sum(derivative[i])
    stiffness = derivative.T @ (weights[:, None] * derivative)

    def interpolate(targets):
        matrix = np.ones((count, count))
        for j in range(count):
            for k in range(count):
                if k != j:
                    matrix[:, j] *= (targets - node_pos[k]) / (node_pos[j] - node_pos[k])
        return matrix

    half_low = interpolate((node_pos - 1.0) / 2.0)
    half_high = interpolate((node_pos + 1.0) / 2.0)
    return tuple(
        (
            jnp.asarray(table, dtype=jnp.float32)
            for table in (weights, stiffness, half_low, half_high)
        )
    )


def face_traces(cube):
    return jnp.stack([cube[0], cube[-1], cube[:, 0], cube[:, -1], cube[:, :, 0], cube[:, :, -1]])


def add_faces(cube, values):
    count = cube.shape[0]
    rest = [(0, 0)] * (cube.ndim - 3)

    def placed(face, axis, at):
        widths = [(0, 0)] * 3
        widths[axis] = (at, count - 1 - at)
        return jnp.pad(jnp.expand_dims(face, axis), widths + rest)

    for index, (axis, at) in enumerate(((0, 0), (0, count - 1), (1, 0), (1, count - 1), (2, 0), (2, count - 1))):
        cube = cube + placed(values[index], axis, at)
    return cube


def orient_faces(neighbour, orientation, subface, half_low, half_high):
    bit_one = (orientation % 2)[:, None, None, :] == 1
    bit_two = (orientation // 2 % 2)[:, None, None, :] == 1
    bit_four = (orientation // 4)[:, None, None, :] == 1
    turned = jnp.where(bit_one, neighbour[:, ::-1], neighbour)
    turned = jnp.where(bit_two, turned[:, :, ::-1], turned)
    turned = jnp.where(bit_four, jnp.swapaxes(turned, 1, 2), turned)
    hanging = (subface > 0)[:, None, None, :]
    quad_first = ((subface - 1) % 2)[:, None, None, :] == 0
    quad_second = ((subface - 1) // 2)[:, None, None, :] == 0
    low_first = jnp.einsum("ai,fibe->fabe", half_low, turned, precision=HIGHEST)
    high_first = jnp.einsum("ai,fibe->fabe", half_high, turned, precision=HIGHEST)
    first_pass = jnp.where(quad_first, low_first, high_first)
    low_second = jnp.einsum("bj,faje->fabe", half_low, first_pass, precision=HIGHEST)
    high_second = jnp.einsum("bj,faje->fabe", half_high, first_pass, precision=HIGHEST)
    second_pass = jnp.where(quad_second, low_second, high_second)
    return jnp.where(hanging, second_pass, turned)


def cell_term(cube, weights, stiffness):
    first_axis = jnp.einsum("ai,ijke->ajke", stiffness, cube, precision=HIGHEST) * (
        weights[None, :, None, None] * weights[None, None, :, None]
    )
    second_axis = jnp.einsum("bj,ijke->ibke", stiffness, cube, precision=HIGHEST) * (
        weights[:, None, None, None] * weights[None, None, :, None]
    )
    third_axis = jnp.einsum("ck,ijke->ijce", stiffness, cube, precision=HIGHEST) * (
        weights[:, None, None, None] * weights[None, :, None, None]
    )
    return first_axis + second_axis + third_axis


def diag_pattern(tables):
    weights, stiffness, half_low, half_high = tables
    count = weights.shape[0]
    stiff_diag = jnp.diagonal(stiffness)
    cell_diag = (
        stiff_diag[:, None, None] * weights[None, :, None] * weights[None, None, :]
        + weights[:, None, None] * stiff_diag[None, :, None] * weights[None, None, :]
        + weights[:, None, None] * weights[None, :, None] * stiff_diag[None, None, :]
    )
    face_mass = PENALTY * weights[:, None] * weights[None, :]
    face_values = jnp.broadcast_to(face_mass[None, :, :, None], (6, count, count, 1))
    pattern = add_faces(cell_diag[:, :, :, None], face_values)
    return pattern.reshape(count * count * count)


def neighbour_traces(traces, face_source, send_list, fields):
    count = traces.shape[1]
    elements = traces.shape[3] // fields
    wide = lax.axis_size("wide")
    rows = fields * count * count
    local = (
        traces.reshape(6, count * count, fields, elements)
        .transpose(2, 1, 0, 3)
        .reshape(rows, 6 * elements)
    )
    picked = local[:, send_list[0]]
    outgoing = picked.T.reshape(3, lax.axis_size("narrow"), -1)
    swapped = lax.all_to_all(outgoing, "narrow", split_axis=1, concat_axis=1, tiled=True)
    up = [(i, i + 1) for i in range(wide - 1)]
    down = [(i + 1, i) for i in range(wide - 1)]
    before = lax.ppermute(swapped[2], "wide", up)
    after = lax.ppermute(swapped[0], "wide", down)
    incoming = jnp.stack([before, swapped[1], after])
    received = incoming.reshape(-1, rows).T
    pool = jnp.concatenate([local, received, jnp.zeros((rows, 1), jnp.float32)], axis=1)
    columns = jnp.where(face_source < 0, pool.shape[1] - 1, face_source).reshape(-1)
    gathered = pool[:, columns]
    return (
        gathered.reshape(fields, count * count, 6, elements)
        .transpose(2, 1, 0, 3)
        .reshape(6, count, count, fields * elements)
    )


def butterfly_sum(value, axis):
    size = lax.axis_size(axis)
    step = 1
    while step < size:
        pairs = [(i, i ^ step) for i in range(size)]
        value = value + lax.ppermute(value, axis, pairs)
        step *= 2
    return value


def chebyshev_coefficients(estimate):
    lam_max = SAFETY * estimate
    lam_min = lam_max / RANGE_RATIO
    theta = (lam_max + lam_min) / 2.0
    delta = (lam_max - lam_min) / 2.0
    sigma = theta / delta
    rho_now = 1.0 / sigma
    zero = jnp.zeros_like(estimate)
    direction = [1.0 / theta] + [zero] * (CHEB - 1)
    solution = list(direction)
    for iteration in range(CHEB - 1):
        scaled_resid = [1.0 - zero] + [-c for c in solution[:-1]]
        rho_new = 1.0 / (2.0 * sigma - rho_now)
        direction = [
            rho_new * rho_now * d + 2.0 * rho_new / delta * r
            for d, r in zip(direction, scaled_resid)
        ]
        solution = [s + d for s, d in zip(solution, direction)]
        rho_now = rho_new
    return solution


def body(rhs, levels, face_source, subface, orientation, send_list, parent, coarse_inverse):
    tables = gll_tables(NODES)
    weights, stiffness, half_low, half_high = tables
    count = NODES
    elements = rhs.shape[1]
    scale = jnp.exp2(-levels.astype(jnp.float32))
    inv_diag = 1.0 / (diag_pattern(tables)[:, None] * scale[None, :])
    face_mass = weights[:, None] * weights[None, :]

    def operator(fields):
        number = len(fields)
        field = jnp.concatenate(fields, axis=1) if number > 1 else fields[0]
        tiled_scale = jnp.tile(scale, number)
        cube = field.reshape(count, count, count, -1)
        traces = face_traces(cube)
        neighbour = orient_faces(
            neighbour_traces(traces, face_source, send_list, number),
            jnp.tile(orientation, (1, number)),
            jnp.tile(subface, (1, number)),
            half_low,
            half_high,
        )
        jumps = PENALTY * face_mass[None, :, :, None] * (traces - neighbour)
        total = add_faces(cell_term(cube, weights, stiffness), jumps)
        total = total.reshape(count * count * count, -1) * tiled_scale[None, :]
        return [total[:, k * elements:(k + 1) * elements] for k in range(number)]

    power = rhs
    krylov = [inv_diag * rhs]
    images = []
    for iteration in range(POWER):
        previous = power
        both = operator([power, krylov[-1]])
        power = inv_diag * both[0]
        images.append(both[1])
        krylov.append(inv_diag * both[1])
    images.append(operator([krylov[-1]])[0])

    mass = (weights[:, None, None] * weights[None, :, None] * weights[None, None, :]).reshape(
        count * count * count, 1
    )
    cells = coarse_inverse.shape[1]
    element_mass = jnp.stack([jnp.sum(mass * v, axis=0) for v in [rhs] + images], axis=1) / 8.0
    partial = jax.ops.segment_sum(element_mass, parent[0], num_segments=cells)
    norms = jnp.stack([jnp.sum(power * power), jnp.sum(previous * previous)])
    block = butterfly_sum(jnp.concatenate([norms, partial.reshape(-1)]), "narrow")
    norms = butterfly_sum(block[:2], "wide")
    restricted = block[2:].reshape(cells, len(images) + 1)

    estimate = jnp.sqrt(norms[0] / norms[1])
    coefficients = chebyshev_coefficients(estimate)
    solution = coefficients[0] * krylov[0]
    applied = coefficients[0] * images[0]
    coarse_res = restricted[:, 0] - coefficients[0] * restricted[:, 1]
    for j in range(1, CHEB):
        solution = solution + coefficients[j] * krylov[j]
        applied = applied + coefficients[j] * images[j]
        coarse_res = coarse_res - coefficients[j] * restricted[:, j + 1]
    residual = rhs - applied
    coarse_cor = jnp.dot(coarse_inverse[0], coarse_res, precision=HIGHEST)
    corrected = solution + coarse_cor[parent[0]][None, :]
    return (corrected, residual)


def solution(mesh):
    in_specs = (
        P(None, ("wide", "narrow")),
        P(("wide", "narrow")),
        P(None, ("wide", "narrow")),
        P(None, ("wide", "narrow")),
        P(None, ("wide", "narrow")),
        P(("wide", "narrow"), None),
        P("wide", "narrow"),
        P("wide", None, None),
    )
    out_specs = (P(None, ("wide", "narrow")), P(None, ("wide", "narrow")))
    return jax.shard_map(body, mesh=mesh, in_specs=in_specs, out_specs=out_specs, check_vma=False)
```

```python
import jax
import jax.numpy as jnp
import numpy as np
from jax import lax
from jax.sharding import PartitionSpec as P

NODES = 8
POWER = 3
CHEB = 4


PENALTY = 32.0
SAFETY = 1.2
RANGE_RATIO = 8.0
HIGHEST = lax.Precision.HIGHEST


def legendre_rows(points, count):
    rows_list = [points * 0.0 + 1.0, points.copy()]
    for order in range(2, count):
        rows_list.append(
            ((2 * order - 1) * points * rows_list[order - 1] - (order - 1) * rows_list[order - 2])
            / order
        )
    return rows_list


def gll_tables(count):
    degree_top = count - 1
    node_pos = np.cos(np.pi * np.arange(count) / degree_top)
    for newton_step in range(60):
        values_table = legendre_rows(node_pos, count)
        node_pos = node_pos - (
            node_pos * values_table[degree_top] - values_table[degree_top - 1]
        ) / (count * values_table[degree_top])
    node_pos = node_pos[::-1].copy()
    node_pos[0] = -1.0
    node_pos[-1] = 1.0
    values_table = legendre_rows(node_pos, count)
    weights = 2.0 / (degree_top * count * values_table[degree_top] ** 2)
    barycentric = np.array(
        [
            1.0 / np.prod([node_pos[j] - node_pos[k] for k in range(count) if k != j])
            for j in range(count)
        ]
    )
    derivative = np.zeros((count, count))
    for i in range(count):
        for j in range(count):
            if i != j:
                derivative[i, j] = barycentric[j] / barycentric[i] / (node_pos[i] - node_pos[j])
        derivative[i, i] = -np.sum(derivative[i])
    stiffness = derivative.T @ (weights[:, None] * derivative)

    def interpolate(targets):
        matrix = np.ones((count, count))
        for j in range(count):
            for k in range(count):
                if k != j:
                    matrix[:, j] *= (targets - node_pos[k]) / (node_pos[j] - node_pos[k])
        return matrix

    half_low = interpolate((node_pos - 1.0) / 2.0)
    half_high = interpolate((node_pos + 1.0) / 2.0)
    return tuple(
        (
            jnp.asarray(table, dtype=jnp.float32)
            for table in (weights, stiffness, half_low, half_high)
        )
    )


def face_traces(cube):
    return jnp.stack([cube[0], cube[-1], cube[:, 0], cube[:, -1], cube[:, :, 0], cube[:, :, -1]])


def add_faces(cube, values):
    count = cube.shape[0]
    first = (jnp.arange(count) == 0).astype(cube.dtype)
    last = (jnp.arange(count) == count - 1).astype(cube.dtype)
    for index in range(6):
        axis, pick = index // 2, (first, last)[index % 2]
        shape = [1] * cube.ndim
        shape[axis] = count
        cube = cube + pick.reshape(shape) * jnp.expand_dims(values[index], axis)
    return cube


def orient_faces(neighbour, orientation, subface, half_low, half_high):
    bit_one = (orientation % 2)[:, None, None, :] == 1
    bit_two = (orientation // 2 % 2)[:, None, None, :] == 1
    bit_four = (orientation // 4)[:, None, None, :] == 1
    turned = jnp.where(bit_one, neighbour[:, ::-1], neighbour)
    turned = jnp.where(bit_two, turned[:, :, ::-1], turned)
    turned = jnp.where(bit_four, jnp.swapaxes(turned, 1, 2), turned)
    hanging = (subface > 0)[:, None, None, :]
    quad_first = ((subface - 1) % 2)[:, None, None, :] == 0
    quad_second = ((subface - 1) // 2)[:, None, None, :] == 0
    low_first = jnp.einsum("ai,fibe->fabe", half_low, turned, precision=HIGHEST)
    high_first = jnp.einsum("ai,fibe->fabe", half_high, turned, precision=HIGHEST)
    first_pass = jnp.where(quad_first, low_first, high_first)
    low_second = jnp.einsum("bj,faje->fabe", half_low, first_pass, precision=HIGHEST)
    high_second = jnp.einsum("bj,faje->fabe", half_high, first_pass, precision=HIGHEST)
    second_pass = jnp.where(quad_second, low_second, high_second)
    return jnp.where(hanging, second_pass, turned)


def cell_term(cube, weights, stiffness):
    first_axis = jnp.einsum("ai,ijke->ajke", stiffness, cube, precision=HIGHEST) * (
        weights[None, :, None, None] * weights[None, None, :, None]
    )
    second_axis = jnp.einsum("bj,ijke->ibke", stiffness, cube, precision=HIGHEST) * (
        weights[:, None, None, None] * weights[None, None, :, None]
    )
    third_axis = jnp.einsum("ck,ijke->ijce", stiffness, cube, precision=HIGHEST) * (
        weights[:, None, None, None] * weights[None, :, None, None]
    )
    return first_axis + second_axis + third_axis


def diag_pattern(tables):
    weights, stiffness, half_low, half_high = tables
    count = weights.shape[0]
    stiff_diag = jnp.diagonal(stiffness)
    cell_diag = (
        stiff_diag[:, None, None] * weights[None, :, None] * weights[None, None, :]
        + weights[:, None, None] * stiff_diag[None, :, None] * weights[None, None, :]
        + weights[:, None, None] * weights[None, :, None] * stiff_diag[None, None, :]
    )
    face_mass = PENALTY * weights[:, None] * weights[None, :]
    face_values = jnp.broadcast_to(face_mass[None, :, :, None], (6, count, count, 1))
    pattern = add_faces(cell_diag[:, :, :, None], face_values)
    return pattern.reshape(count * count * count)


def neighbour_traces(traces, face_source, send_list, fields):
    count = traces.shape[1]
    elements = traces.shape[3] // fields
    wide = lax.axis_size("wide")
    rows = fields * count * count
    local = (
        traces.reshape(6, count * count, fields, elements)
        .transpose(2, 1, 0, 3)
        .reshape(rows, 6 * elements)
    )
    picked = local[:, send_list[0]]
    outgoing = picked.T.reshape(3, lax.axis_size("narrow"), -1)
    swapped = lax.all_to_all(outgoing, "narrow", split_axis=1, concat_axis=1, tiled=True)
    up = [(i, i + 1) for i in range(wide - 1)]
    down = [(i + 1, i) for i in range(wide - 1)]
    before = lax.ppermute(swapped[2], "wide", up)
    after = lax.ppermute(swapped[0], "wide", down)
    incoming = jnp.stack([before, swapped[1], after])
    received = incoming.reshape(-1, rows).T
    pool = jnp.concatenate([local, received, jnp.zeros((rows, 1), jnp.float32)], axis=1)
    columns = jnp.where(face_source < 0, pool.shape[1] - 1, face_source).reshape(-1)
    gathered = pool[:, columns]
    return (
        gathered.reshape(fields, count * count, 6, elements)
        .transpose(2, 1, 0, 3)
        .reshape(6, count, count, fields * elements)
    )


def chebyshev_coefficients(estimate):
    lam_max = SAFETY * estimate
    lam_min = lam_max / RANGE_RATIO
    theta = (lam_max + lam_min) / 2.0
    delta = (lam_max - lam_min) / 2.0
    sigma = theta / delta
    rho_now = 1.0 / sigma
    zero = jnp.zeros_like(estimate)
    direction = [1.0 / theta] + [zero] * (CHEB - 1)
    solution = list(direction)
    for iteration in range(CHEB - 1):
        scaled_resid = [1.0 - zero] + [-c for c in solution[:-1]]
        rho_new = 1.0 / (2.0 * sigma - rho_now)
        direction = [
            rho_new * rho_now * d + 2.0 * rho_new / delta * r
            for d, r in zip(direction, scaled_resid)
        ]
        solution = [s + d for s, d in zip(solution, direction)]
        rho_now = rho_new
    return solution


def body(rhs, levels, face_source, subface, orientation, send_list, parent, coarse_inverse):
    tables = gll_tables(NODES)
    weights, stiffness, half_low, half_high = tables
    count = NODES
    elements = rhs.shape[1]
    scale = jnp.exp2(-levels.astype(jnp.float32))
    inv_diag = 1.0 / (diag_pattern(tables)[:, None] * scale[None, :])
    face_mass = weights[:, None] * weights[None, :]

    def operator(fields):
        number = len(fields)
        field = jnp.concatenate(fields, axis=1) if number > 1 else fields[0]
        tiled_scale = jnp.tile(scale, number)
        cube = field.reshape(count, count, count, -1)
        traces = face_traces(cube)
        neighbour = orient_faces(
            neighbour_traces(traces, face_source, send_list, number),
            jnp.tile(orientation, (1, number)),
            jnp.tile(subface, (1, number)),
            half_low,
            half_high,
        )
        jumps = PENALTY * face_mass[None, :, :, None] * (traces - neighbour)
        total = add_faces(cell_term(cube, weights, stiffness), jumps)
        total = total.reshape(count * count * count, -1) * tiled_scale[None, :]
        return [total[:, k * elements:(k + 1) * elements] for k in range(number)]

    power = rhs
    krylov = [inv_diag * rhs]
    images = []
    for iteration in range(POWER):
        previous = power
        both = operator([power, krylov[-1]])
        power = inv_diag * both[0]
        images.append(both[1])
        krylov.append(inv_diag * both[1])
    images.append(operator([krylov[-1]])[0])

    mass = (weights[:, None, None] * weights[None, :, None] * weights[None, None, :]).reshape(
        count * count * count, 1
    )
    cells = coarse_inverse.shape[1]
    element_mass = jnp.stack([jnp.sum(mass * v, axis=0) for v in [rhs] + images], axis=1) / 8.0
    partial = jax.ops.segment_sum(element_mass, parent[0], num_segments=cells)
    norms = jnp.stack([jnp.sum(power * power), jnp.sum(previous * previous)])
    block = lax.psum(jnp.concatenate([norms, partial.reshape(-1)]), "narrow")
    wide = lax.axis_size("wide")
    spread = jnp.broadcast_to(block[None, :2], (wide, 2))
    norms = jnp.sum(lax.all_to_all(spread, "wide", 0, 0, tiled=True), axis=0)
    restricted = block[2:].reshape(cells, len(images) + 1)

    estimate = jnp.sqrt(norms[0] / norms[1])
    coefficients = chebyshev_coefficients(estimate)
    solution = coefficients[0] * krylov[0]
    applied = coefficients[0] * images[0]
    coarse_res = restricted[:, 0] - coefficients[0] * restricted[:, 1]
    for j in range(1, CHEB):
        solution = solution + coefficients[j] * krylov[j]
        applied = applied + coefficients[j] * images[j]
        coarse_res = coarse_res - coefficients[j] * restricted[:, j + 1]
    residual = rhs - applied
    coarse_cor = jnp.dot(coarse_inverse[0], coarse_res, precision=HIGHEST)
    corrected = solution + coarse_cor[parent[0]][None, :]
    return (corrected, residual)


def solution(mesh):
    in_specs = (
        P(None, ("wide", "narrow")),
        P(("wide", "narrow")),
        P(None, ("wide", "narrow")),
        P(None, ("wide", "narrow")),
        P(None, ("wide", "narrow")),
        P(("wide", "narrow"), None),
        P("wide", "narrow"),
        P("wide", None, None),
    )
    out_specs = (P(None, ("wide", "narrow")), P(None, ("wide", "narrow")))
    return jax.shard_map(body, mesh=mesh, in_specs=in_specs, out_specs=out_specs, check_vma=False)
```

```python
import jax
import jax.numpy as jnp
import numpy as np
from jax import lax
from jax.sharding import PartitionSpec as P

NODES = 8
POWER = 3
CHEB = 4


PENALTY = 32.0
SAFETY = 1.2
RANGE_RATIO = 8.0
HIGHEST = lax.Precision.HIGHEST


def legendre_rows(points, count):
    rows_list = [points * 0.0 + 1.0, points.copy()]
    for order in range(2, count):
        rows_list.append(
            ((2 * order - 1) * points * rows_list[order - 1] - (order - 1) * rows_list[order - 2])
            / order
        )
    return rows_list


def gll_tables(count):
    degree_top = count - 1
    node_pos = np.cos(np.pi * np.arange(count) / degree_top)
    for newton_step in range(60):
        values_table = legendre_rows(node_pos, count)
        node_pos = node_pos - (
            node_pos * values_table[degree_top] - values_table[degree_top - 1]
        ) / (count * values_table[degree_top])
    node_pos = node_pos[::-1].copy()
    node_pos[0] = -1.0
    node_pos[-1] = 1.0
    values_table = legendre_rows(node_pos, count)
    weights = 2.0 / (degree_top * count * values_table[degree_top] ** 2)
    barycentric = np.array(
        [
            1.0 / np.prod([node_pos[j] - node_pos[k] for k in range(count) if k != j])
            for j in range(count)
        ]
    )
    derivative = np.zeros((count, count))
    for i in range(count):
        for j in range(count):
            if i != j:
                derivative[i, j] = barycentric[j] / barycentric[i] / (node_pos[i] - node_pos[j])
        derivative[i, i] = -np.sum(derivative[i])
    stiffness = derivative.T @ (weights[:, None] * derivative)

    def interpolate(targets):
        matrix = np.ones((count, count))
        for j in range(count):
            for k in range(count):
                if k != j:
                    matrix[:, j] *= (targets - node_pos[k]) / (node_pos[j] - node_pos[k])
        return matrix

    half_low = interpolate((node_pos - 1.0) / 2.0)
    half_high = interpolate((node_pos + 1.0) / 2.0)
    return tuple(
        (
            np.asarray(table, dtype=np.float32)
            for table in (weights, stiffness, half_low, half_high)
        )
    )


def face_traces(cube):
    return jnp.stack([cube[0], cube[-1], cube[:, 0], cube[:, -1], cube[:, :, 0], cube[:, :, -1]])


def add_faces(cube, values):
    count = cube.shape[0]
    first = (jnp.arange(count) == 0).astype(cube.dtype)
    last = (jnp.arange(count) == count - 1).astype(cube.dtype)
    for index in range(6):
        axis, pick = index // 2, (first, last)[index % 2]
        shape = [1] * cube.ndim
        shape[axis] = count
        cube = cube + pick.reshape(shape) * jnp.expand_dims(values[index], axis)
    return cube


def orient_faces(neighbour, orientation, subface, half_low, half_high):
    bit_one = (orientation % 2)[:, None, None, :] == 1
    bit_two = (orientation // 2 % 2)[:, None, None, :] == 1
    bit_four = (orientation // 4)[:, None, None, :] == 1
    turned = jnp.where(bit_one, neighbour[:, ::-1], neighbour)
    turned = jnp.where(bit_two, turned[:, :, ::-1], turned)
    turned = jnp.where(bit_four, jnp.swapaxes(turned, 1, 2), turned)
    hanging = (subface > 0)[:, None, None, :]
    quad_first = ((subface - 1) % 2)[:, None, None, :] == 0
    quad_second = ((subface - 1) // 2)[:, None, None, :] == 0
    low_first = jnp.einsum("ai,fibe->fabe", half_low, turned, precision=HIGHEST)
    high_first = jnp.einsum("ai,fibe->fabe", half_high, turned, precision=HIGHEST)
    first_pass = jnp.where(quad_first, low_first, high_first)
    low_second = jnp.einsum("bj,faje->fabe", half_low, first_pass, precision=HIGHEST)
    high_second = jnp.einsum("bj,faje->fabe", half_high, first_pass, precision=HIGHEST)
    second_pass = jnp.where(quad_second, low_second, high_second)
    return jnp.where(hanging, second_pass, turned)


def cell_term(cube, weights, stiffness):
    first_axis = jnp.einsum("ai,ijke->ajke", stiffness, cube, precision=HIGHEST) * (
        weights[None, :, None, None] * weights[None, None, :, None]
    )
    second_axis = jnp.einsum("bj,ijke->ibke", stiffness, cube, precision=HIGHEST) * (
        weights[:, None, None, None] * weights[None, None, :, None]
    )
    third_axis = jnp.einsum("ck,ijke->ijce", stiffness, cube, precision=HIGHEST) * (
        weights[:, None, None, None] * weights[None, :, None, None]
    )
    return first_axis + second_axis + third_axis


def diag_pattern(tables):
    weights, stiffness, half_low, half_high = tables
    count = weights.shape[0]
    stiff_diag = jnp.diagonal(stiffness)
    cell_diag = (
        stiff_diag[:, None, None] * weights[None, :, None] * weights[None, None, :]
        + weights[:, None, None] * stiff_diag[None, :, None] * weights[None, None, :]
        + weights[:, None, None] * weights[None, :, None] * stiff_diag[None, None, :]
    )
    face_mass = PENALTY * weights[:, None] * weights[None, :]
    face_values = jnp.broadcast_to(face_mass[None, :, :, None], (6, count, count, 1))
    pattern = add_faces(cell_diag[:, :, :, None], face_values)
    return pattern.reshape(count * count * count)


def operator_matrices(weights, stiffness):
    w = np.asarray(weights, np.float64)
    stiff = np.asarray(stiffness, np.float64)
    count = w.shape[0]
    mass = np.diag(w)
    cell = (
        np.kron(np.kron(stiff, mass), mass)
        + np.kron(np.kron(mass, stiff), mass)
        + np.kron(np.kron(mass, mass), stiff)
    )
    place = np.zeros((count ** 3, 6, count, count))
    for r in range(count):
        for s in range(count):
            weight = PENALTY * w[r] * w[s]
            for face, (i, j, k) in enumerate(
                ((0, r, s), (count - 1, r, s), (r, 0, s), (r, count - 1, s), (r, s, 0), (r, s, count - 1))
            ):
                place[(i * count + j) * count + k, face, r, s] = weight
    return (
        jnp.asarray(cell, dtype=jnp.float32),
        jnp.asarray(place.reshape(count ** 3, 6 * count * count), dtype=jnp.float32),
    )


def neighbour_traces(traces, face_source, send_list, fields):
    count = traces.shape[1]
    elements = traces.shape[3] // fields
    wide = lax.axis_size("wide")
    rows = fields * count * count
    local = (
        traces.reshape(6, count * count, fields, elements)
        .transpose(2, 1, 0, 3)
        .reshape(rows, 6 * elements)
    )
    picked = local[:, send_list[0]]
    outgoing = picked.T.reshape(3, lax.axis_size("narrow"), -1)
    swapped = lax.all_to_all(outgoing, "narrow", split_axis=1, concat_axis=1, tiled=True)
    up = [(i, i + 1) for i in range(wide - 1)]
    down = [(i + 1, i) for i in range(wide - 1)]
    before = lax.ppermute(swapped[2], "wide", up)
    after = lax.ppermute(swapped[0], "wide", down)
    incoming = jnp.stack([before, swapped[1], after])
    received = incoming.reshape(-1, rows).T
    pool = jnp.concatenate([local, received, jnp.zeros((rows, 1), jnp.float32)], axis=1)
    columns = jnp.where(face_source < 0, pool.shape[1] - 1, face_source).reshape(-1)
    gathered = pool[:, columns]
    return (
        gathered.reshape(fields, count * count, 6, elements)
        .transpose(2, 1, 0, 3)
        .reshape(6, count, count, fields * elements)
    )


def chebyshev_coefficients(estimate):
    lam_max = SAFETY * estimate
    lam_min = lam_max / RANGE_RATIO
    theta = (lam_max + lam_min) / 2.0
    delta = (lam_max - lam_min) / 2.0
    sigma = theta / delta
    rho_now = 1.0 / sigma
    zero = jnp.zeros_like(estimate)
    direction = [1.0 / theta] + [zero] * (CHEB - 1)
    solution = list(direction)
    for iteration in range(CHEB - 1):
        scaled_resid = [1.0 - zero] + [-c for c in solution[:-1]]
        rho_new = 1.0 / (2.0 * sigma - rho_now)
        direction = [
            rho_new * rho_now * d + 2.0 * rho_new / delta * r
            for d, r in zip(direction, scaled_resid)
        ]
        solution = [s + d for s, d in zip(solution, direction)]
        rho_now = rho_new
    return solution


def body(rhs, levels, face_source, subface, orientation, send_list, parent, coarse_inverse):
    tables = gll_tables(NODES)
    weights, stiffness, half_low, half_high = tables
    count = NODES
    elements = rhs.shape[1]
    scale = jnp.exp2(-levels.astype(jnp.float32))
    inv_diag = 1.0 / (diag_pattern(tables)[:, None] * scale[None, :])
    cell_matrix, place_matrix = operator_matrices(weights, stiffness)

    def operator(fields):
        number = len(fields)
        field = jnp.concatenate(fields, axis=1) if number > 1 else fields[0]
        tiled_scale = jnp.tile(scale, number)
        cube = field.reshape(count, count, count, -1)
        traces = face_traces(cube)
        neighbour = orient_faces(
            neighbour_traces(traces, face_source, send_list, number),
            jnp.tile(orientation, (1, number)),
            jnp.tile(subface, (1, number)),
            half_low,
            half_high,
        )
        jumps = (traces - neighbour).reshape(6 * count * count, -1)
        total = jnp.dot(cell_matrix, field, precision=HIGHEST) + jnp.dot(
            place_matrix, jumps, precision=HIGHEST
        )
        total = total * tiled_scale[None, :]
        return [total[:, k * elements:(k + 1) * elements] for k in range(number)]

    power = rhs
    krylov = [inv_diag * rhs]
    images = []
    for iteration in range(POWER):
        previous = power
        both = operator([power, krylov[-1]])
        power = inv_diag * both[0]
        images.append(both[1])
        krylov.append(inv_diag * both[1])
    images.append(operator([krylov[-1]])[0])

    mass = (weights[:, None, None] * weights[None, :, None] * weights[None, None, :]).reshape(
        count * count * count, 1
    )
    cells = coarse_inverse.shape[1]
    element_mass = jnp.stack([jnp.sum(mass * v, axis=0) for v in [rhs] + images], axis=1) / 8.0
    partial = jax.ops.segment_sum(element_mass, parent[0], num_segments=cells)
    norms = jnp.stack([jnp.sum(power * power), jnp.sum(previous * previous)])
    block = lax.psum(jnp.concatenate([norms, partial.reshape(-1)]), "narrow")
    wide = lax.axis_size("wide")
    spread = jnp.broadcast_to(block[None, :2], (wide, 2))
    norms = jnp.sum(lax.all_to_all(spread, "wide", 0, 0, tiled=True), axis=0)
    restricted = block[2:].reshape(cells, len(images) + 1)

    estimate = jnp.sqrt(norms[0] / norms[1])
    coefficients = chebyshev_coefficients(estimate)
    solution = coefficients[0] * krylov[0]
    applied = coefficients[0] * images[0]
    coarse_res = restricted[:, 0] - coefficients[0] * restricted[:, 1]
    for j in range(1, CHEB):
        solution = solution + coefficients[j] * krylov[j]
        applied = applied + coefficients[j] * images[j]
        coarse_res = coarse_res - coefficients[j] * restricted[:, j + 1]
    residual = rhs - applied
    coarse_cor = jnp.dot(coarse_inverse[0], coarse_res, precision=HIGHEST)
    corrected = solution + coarse_cor[parent[0]][None, :]
    return (corrected, residual)


def solution(mesh):
    in_specs = (
        P(None, ("wide", "narrow")),
        P(("wide", "narrow")),
        P(None, ("wide", "narrow")),
        P(None, ("wide", "narrow")),
        P(None, ("wide", "narrow")),
        P(("wide", "narrow"), None),
        P("wide", "narrow"),
        P("wide", None, None),
    )
    out_specs = (P(None, ("wide", "narrow")), P(None, ("wide", "narrow")))
    return jax.shard_map(body, mesh=mesh, in_specs=in_specs, out_specs=out_specs, check_vma=False)
```

```python
import jax
import jax.numpy as jnp
import numpy as np
from jax import lax
from jax.sharding import PartitionSpec as P

NODES = 8
POWER = 3
CHEB = 4


PENALTY = 32.0
SAFETY = 1.2
RANGE_RATIO = 8.0
HIGHEST = lax.Precision.HIGHEST


def legendre_rows(points, count):
    rows_list = [points * 0.0 + 1.0, points.copy()]
    for order in range(2, count):
        rows_list.append(
            ((2 * order - 1) * points * rows_list[order - 1] - (order - 1) * rows_list[order - 2])
            / order
        )
    return rows_list


def gll_tables(count):
    degree_top = count - 1
    node_pos = np.cos(np.pi * np.arange(count) / degree_top)
    for newton_step in range(60):
        values_table = legendre_rows(node_pos, count)
        node_pos = node_pos - (
            node_pos * values_table[degree_top] - values_table[degree_top - 1]
        ) / (count * values_table[degree_top])
    node_pos = node_pos[::-1].copy()
    node_pos[0] = -1.0
    node_pos[-1] = 1.0
    values_table = legendre_rows(node_pos, count)
    weights = 2.0 / (degree_top * count * values_table[degree_top] ** 2)
    barycentric = np.array(
        [
            1.0 / np.prod([node_pos[j] - node_pos[k] for k in range(count) if k != j])
            for j in range(count)
        ]
    )
    derivative = np.zeros((count, count))
    for i in range(count):
        for j in range(count):
            if i != j:
                derivative[i, j] = barycentric[j] / barycentric[i] / (node_pos[i] - node_pos[j])
        derivative[i, i] = -np.sum(derivative[i])
    stiffness = derivative.T @ (weights[:, None] * derivative)

    def interpolate(targets):
        matrix = np.ones((count, count))
        for j in range(count):
            for k in range(count):
                if k != j:
                    matrix[:, j] *= (targets - node_pos[k]) / (node_pos[j] - node_pos[k])
        return matrix

    half_low = interpolate((node_pos - 1.0) / 2.0)
    half_high = interpolate((node_pos + 1.0) / 2.0)
    return tuple(
        (
            jnp.asarray(table, dtype=jnp.float32)
            for table in (weights, stiffness, half_low, half_high)
        )
    )


def face_traces(cube):
    return jnp.stack([cube[0], cube[-1], cube[:, 0], cube[:, -1], cube[:, :, 0], cube[:, :, -1]])


def add_faces(cube, values):
    count = cube.shape[0]
    first = (jnp.arange(count) == 0).astype(cube.dtype)
    last = (jnp.arange(count) == count - 1).astype(cube.dtype)
    for index in range(6):
        axis, pick = index // 2, (first, last)[index % 2]
        shape = [1] * cube.ndim
        shape[axis] = count
        cube = cube + pick.reshape(shape) * jnp.expand_dims(values[index], axis)
    return cube


def orient_faces(neighbour, orientation, subface, half_low, half_high):
    bit_one = (orientation % 2)[:, None, None, :] == 1
    bit_two = (orientation // 2 % 2)[:, None, None, :] == 1
    bit_four = (orientation // 4)[:, None, None, :] == 1
    turned = jnp.where(bit_one, neighbour[:, ::-1], neighbour)
    turned = jnp.where(bit_two, turned[:, :, ::-1], turned)
    turned = jnp.where(bit_four, jnp.swapaxes(turned, 1, 2), turned)
    hanging = (subface > 0)[:, None, None, :]
    quad_first = ((subface - 1) % 2)[:, None, None, :] == 0
    quad_second = ((subface - 1) // 2)[:, None, None, :] == 0
    low_first = jnp.einsum("ai,fibe->fabe", half_low, turned, precision=HIGHEST)
    high_first = jnp.einsum("ai,fibe->fabe", half_high, turned, precision=HIGHEST)
    first_pass = jnp.where(quad_first, low_first, high_first)
    low_second = jnp.einsum("bj,faje->fabe", half_low, first_pass, precision=HIGHEST)
    high_second = jnp.einsum("bj,faje->fabe", half_high, first_pass, precision=HIGHEST)
    second_pass = jnp.where(quad_second, low_second, high_second)
    return jnp.where(hanging, second_pass, turned)


def cell_term(cube, weights, stiffness):
    first_axis = jnp.einsum("ai,ijke->ajke", stiffness, cube, precision=HIGHEST) * (
        weights[None, :, None, None] * weights[None, None, :, None]
    )
    second_axis = jnp.einsum("bj,ijke->ibke", stiffness, cube, precision=HIGHEST) * (
        weights[:, None, None, None] * weights[None, None, :, None]
    )
    third_axis = jnp.einsum("ck,ijke->ijce", stiffness, cube, precision=HIGHEST) * (
        weights[:, None, None, None] * weights[None, :, None, None]
    )
    return first_axis + second_axis + third_axis


def diag_pattern(tables):
    weights, stiffness, half_low, half_high = tables
    count = weights.shape[0]
    stiff_diag = jnp.diagonal(stiffness)
    cell_diag = (
        stiff_diag[:, None, None] * weights[None, :, None] * weights[None, None, :]
        + weights[:, None, None] * stiff_diag[None, :, None] * weights[None, None, :]
        + weights[:, None, None] * weights[None, :, None] * stiff_diag[None, None, :]
    )
    face_mass = PENALTY * weights[:, None] * weights[None, :]
    face_values = jnp.broadcast_to(face_mass[None, :, :, None], (6, count, count, 1))
    pattern = add_faces(cell_diag[:, :, :, None], face_values)
    return pattern.reshape(count * count * count)


def neighbour_traces(traces, face_source, send_list, fields):
    count = traces.shape[1]
    elements = traces.shape[3] // fields
    wide = lax.axis_size("wide")
    rows = fields * count * count
    local = (
        traces.reshape(6, count * count, fields, elements)
        .transpose(2, 1, 0, 3)
        .reshape(rows, 6 * elements)
    )
    picked = local[:, send_list[0]]
    outgoing = picked.T.reshape(3, lax.axis_size("narrow"), -1)
    swapped = lax.all_to_all(outgoing, "narrow", split_axis=1, concat_axis=1, tiled=True)
    up = [(i, i + 1) for i in range(wide - 1)]
    down = [(i + 1, i) for i in range(wide - 1)]
    before = lax.ppermute(swapped[2], "wide", up)
    after = lax.ppermute(swapped[0], "wide", down)
    incoming = jnp.stack([before, swapped[1], after])
    received = incoming.reshape(-1, rows).T
    pool = jnp.concatenate([local, received, jnp.zeros((rows, 1), jnp.float32)], axis=1)
    columns = jnp.where(face_source < 0, pool.shape[1] - 1, face_source).reshape(-1)
    gathered = pool[:, columns]
    return (
        gathered.reshape(fields, count * count, 6, elements)
        .transpose(2, 1, 0, 3)
        .reshape(6, count, count, fields * elements)
    )


def chebyshev_coefficients(estimate):
    lam_max = SAFETY * estimate
    lam_min = lam_max / RANGE_RATIO
    theta = (lam_max + lam_min) / 2.0
    delta = (lam_max - lam_min) / 2.0
    sigma = theta / delta
    rho_now = 1.0 / sigma
    zero = jnp.zeros_like(estimate)
    direction = [1.0 / theta] + [zero] * (CHEB - 1)
    solution = list(direction)
    for iteration in range(CHEB - 1):
        scaled_resid = [1.0 - zero] + [-c for c in solution[:-1]]
        rho_new = 1.0 / (2.0 * sigma - rho_now)
        direction = [
            rho_new * rho_now * d + 2.0 * rho_new / delta * r
            for d, r in zip(direction, scaled_resid)
        ]
        solution = [s + d for s, d in zip(solution, direction)]
        rho_now = rho_new
    return solution


def body(rhs, levels, face_source, subface, orientation, send_list, parent, coarse_inverse):
    tables = gll_tables(NODES)
    weights, stiffness, half_low, half_high = tables
    count = NODES
    elements = rhs.shape[1]
    scale = jnp.exp2(-levels.astype(jnp.float32))
    inv_diag = 1.0 / (diag_pattern(tables)[:, None] * scale[None, :])
    face_mass = weights[:, None] * weights[None, :]

    def operator(fields):
        number = len(fields)
        field = jnp.concatenate(fields, axis=1) if number > 1 else fields[0]
        tiled_scale = jnp.tile(scale, number)
        cube = field.reshape(count, count, count, -1)
        traces = face_traces(cube)
        neighbour = orient_faces(
            neighbour_traces(traces, face_source, send_list, number),
            jnp.tile(orientation, (1, number)),
            jnp.tile(subface, (1, number)),
            half_low,
            half_high,
        )
        jumps = PENALTY * face_mass[None, :, :, None] * (traces - neighbour)
        total = add_faces(cell_term(cube, weights, stiffness), jumps)
        total = total.reshape(count * count * count, -1) * tiled_scale[None, :]
        return [total[:, k * elements:(k + 1) * elements] for k in range(number)]

    def paired_round(iteration, carry):
        power, previous, latest, krylov_stack, image_stack = carry
        both = operator([power, latest])
        latest = inv_diag * both[1]
        return (
            inv_diag * both[0],
            power,
            latest,
            lax.dynamic_update_index_in_dim(krylov_stack, latest, iteration, 0),
            lax.dynamic_update_index_in_dim(image_stack, both[1], iteration, 0),
        )

    start = inv_diag * rhs
    history = jnp.zeros((POWER,) + rhs.shape, rhs.dtype)
    power, previous, latest, krylov_stack, image_stack = lax.fori_loop(
        0, POWER, paired_round, (rhs, rhs, start, history, history)
    )
    krylov = [start] + [krylov_stack[j] for j in range(POWER)]
    images = [image_stack[j] for j in range(POWER)] + [operator([latest])[0]]

    mass = (weights[:, None, None] * weights[None, :, None] * weights[None, None, :]).reshape(
        count * count * count, 1
    )
    cells = coarse_inverse.shape[1]
    element_mass = jnp.stack([jnp.sum(mass * v, axis=0) for v in [rhs] + images], axis=1) / 8.0
    partial = jax.ops.segment_sum(element_mass, parent[0], num_segments=cells)
    norms = jnp.stack([jnp.sum(power * power), jnp.sum(previous * previous)])
    block = lax.psum(jnp.concatenate([norms, partial.reshape(-1)]), "narrow")
    wide = lax.axis_size("wide")
    spread = jnp.broadcast_to(block[None, :2], (wide, 2))
    norms = jnp.sum(lax.all_to_all(spread, "wide", 0, 0, tiled=True), axis=0)
    restricted = block[2:].reshape(cells, len(images) + 1)

    estimate = jnp.sqrt(norms[0] / norms[1])
    coefficients = chebyshev_coefficients(estimate)
    solution = coefficients[0] * krylov[0]
    applied = coefficients[0] * images[0]
    coarse_res = restricted[:, 0] - coefficients[0] * restricted[:, 1]
    for j in range(1, CHEB):
        solution = solution + coefficients[j] * krylov[j]
        applied = applied + coefficients[j] * images[j]
        coarse_res = coarse_res - coefficients[j] * restricted[:, j + 1]
    residual = rhs - applied
    coarse_cor = jnp.dot(coarse_inverse[0], coarse_res, precision=HIGHEST)
    corrected = solution + coarse_cor[parent[0]][None, :]
    return (corrected, residual)


def solution(mesh):
    in_specs = (
        P(None, ("wide", "narrow")),
        P(("wide", "narrow")),
        P(None, ("wide", "narrow")),
        P(None, ("wide", "narrow")),
        P(None, ("wide", "narrow")),
        P(("wide", "narrow"), None),
        P("wide", "narrow"),
        P("wide", None, None),
    )
    out_specs = (P(None, ("wide", "narrow")), P(None, ("wide", "narrow")))
    return jax.shard_map(body, mesh=mesh, in_specs=in_specs, out_specs=out_specs, check_vma=False)
```

```python
import jax
import jax.numpy as jnp
import numpy as np
from jax import lax
from jax.sharding import PartitionSpec as P

NODES = 8
POWER = 3
CHEB = 4


PENALTY = 32.0
SAFETY = 1.2
RANGE_RATIO = 8.0
HIGHEST = lax.Precision.HIGHEST


def legendre_rows(points, count):
    rows_list = [points * 0.0 + 1.0, points.copy()]
    for order in range(2, count):
        rows_list.append(
            ((2 * order - 1) * points * rows_list[order - 1] - (order - 1) * rows_list[order - 2])
            / order
        )
    return rows_list


def gll_tables(count):
    degree_top = count - 1
    node_pos = np.cos(np.pi * np.arange(count) / degree_top)
    for newton_step in range(60):
        values_table = legendre_rows(node_pos, count)
        node_pos = node_pos - (
            node_pos * values_table[degree_top] - values_table[degree_top - 1]
        ) / (count * values_table[degree_top])
    node_pos = node_pos[::-1].copy()
    node_pos[0] = -1.0
    node_pos[-1] = 1.0
    values_table = legendre_rows(node_pos, count)
    weights = 2.0 / (degree_top * count * values_table[degree_top] ** 2)
    barycentric = np.array(
        [
            1.0 / np.prod([node_pos[j] - node_pos[k] for k in range(count) if k != j])
            for j in range(count)
        ]
    )
    derivative = np.zeros((count, count))
    for i in range(count):
        for j in range(count):
            if i != j:
                derivative[i, j] = barycentric[j] / barycentric[i] / (node_pos[i] - node_pos[j])
        derivative[i, i] = -np.sum(derivative[i])
    stiffness = derivative.T @ (weights[:, None] * derivative)

    def interpolate(targets):
        matrix = np.ones((count, count))
        for j in range(count):
            for k in range(count):
                if k != j:
                    matrix[:, j] *= (targets - node_pos[k]) / (node_pos[j] - node_pos[k])
        return matrix

    half_low = interpolate((node_pos - 1.0) / 2.0)
    half_high = interpolate((node_pos + 1.0) / 2.0)
    return tuple(
        (
            jnp.asarray(table, dtype=jnp.float32)
            for table in (weights, stiffness, half_low, half_high)
        )
    )


def face_traces(cube):
    return jnp.stack([cube[0], cube[-1], cube[:, 0], cube[:, -1], cube[:, :, 0], cube[:, :, -1]])


def add_faces(cube, values):
    count = cube.shape[0]
    first = (jnp.arange(count) == 0).astype(cube.dtype)
    last = (jnp.arange(count) == count - 1).astype(cube.dtype)
    for index in range(6):
        axis, pick = index // 2, (first, last)[index % 2]
        shape = [1] * cube.ndim
        shape[axis] = count
        cube = cube + pick.reshape(shape) * jnp.expand_dims(values[index], axis)
    return cube


def orient_faces(neighbour, orientation, subface, half_low, half_high):
    bit_one = (orientation % 2)[:, None, None, :] == 1
    bit_two = (orientation // 2 % 2)[:, None, None, :] == 1
    bit_four = (orientation // 4)[:, None, None, :] == 1
    turned = jnp.where(bit_one, neighbour[:, ::-1], neighbour)
    turned = jnp.where(bit_two, turned[:, :, ::-1], turned)
    turned = jnp.where(bit_four, jnp.swapaxes(turned, 1, 2), turned)
    hanging = (subface > 0)[:, None, None, :]
    quad_first = ((subface - 1) % 2)[:, None, None, :] == 0
    quad_second = ((subface - 1) // 2)[:, None, None, :] == 0
    low_first = jnp.einsum("ai,fibe->fabe", half_low, turned, precision=HIGHEST)
    high_first = jnp.einsum("ai,fibe->fabe", half_high, turned, precision=HIGHEST)
    first_pass = jnp.where(quad_first, low_first, high_first)
    low_second = jnp.einsum("bj,faje->fabe", half_low, first_pass, precision=HIGHEST)
    high_second = jnp.einsum("bj,faje->fabe", half_high, first_pass, precision=HIGHEST)
    second_pass = jnp.where(quad_second, low_second, high_second)
    return jnp.where(hanging, second_pass, turned)


def cell_term(cube, weights, stiffness):
    first_axis = jnp.einsum("ai,ijke->ajke", stiffness, cube, precision=HIGHEST) * (
        weights[None, :, None, None] * weights[None, None, :, None]
    )
    second_axis = jnp.einsum("bj,ijke->ibke", stiffness, cube, precision=HIGHEST) * (
        weights[:, None, None, None] * weights[None, None, :, None]
    )
    third_axis = jnp.einsum("ck,ijke->ijce", stiffness, cube, precision=HIGHEST) * (
        weights[:, None, None, None] * weights[None, :, None, None]
    )
    return first_axis + second_axis + third_axis


def diag_pattern(tables):
    weights, stiffness, half_low, half_high = tables
    count = weights.shape[0]
    stiff_diag = jnp.diagonal(stiffness)
    cell_diag = (
        stiff_diag[:, None, None] * weights[None, :, None] * weights[None, None, :]
        + weights[:, None, None] * stiff_diag[None, :, None] * weights[None, None, :]
        + weights[:, None, None] * weights[None, :, None] * stiff_diag[None, None, :]
    )
    face_mass = PENALTY * weights[:, None] * weights[None, :]
    face_values = jnp.broadcast_to(face_mass[None, :, :, None], (6, count, count, 1))
    pattern = add_faces(cell_diag[:, :, :, None], face_values)
    return pattern.reshape(count * count * count)


def neighbour_traces(traces, face_source, send_list, fields):
    count = traces.shape[1]
    elements = traces.shape[3] // fields
    wide = lax.axis_size("wide")
    rows = fields * count * count
    local = (
        traces.reshape(6, count * count, fields, elements)
        .transpose(2, 1, 0, 3)
        .reshape(rows, 6 * elements)
    )
    picked = local[:, send_list[0]]
    outgoing = picked.T.reshape(3, lax.axis_size("narrow"), -1)
    swapped = lax.all_to_all(outgoing, "narrow", split_axis=1, concat_axis=1, tiled=True)
    up = [(i, i + 1) for i in range(wide - 1)]
    down = [(i + 1, i) for i in range(wide - 1)]
    before = lax.ppermute(swapped[2], "wide", up)
    after = lax.ppermute(swapped[0], "wide", down)
    incoming = jnp.stack([before, swapped[1], after])
    received = incoming.reshape(-1, rows).T
    pool = jnp.concatenate([local, received, jnp.zeros((rows, 1), jnp.float32)], axis=1)
    columns = jnp.where(face_source < 0, pool.shape[1] - 1, face_source).reshape(-1)
    gathered = pool[:, columns]
    return (
        gathered.reshape(fields, count * count, 6, elements)
        .transpose(2, 1, 0, 3)
        .reshape(6, count, count, fields * elements)
    )


def chebyshev_coefficients(estimate):
    lam_max = SAFETY * estimate
    lam_min = lam_max / RANGE_RATIO
    theta = (lam_max + lam_min) / 2.0
    delta = (lam_max - lam_min) / 2.0
    sigma = theta / delta
    rho_now = 1.0 / sigma
    zero = jnp.zeros_like(estimate)
    direction = [1.0 / theta] + [zero] * (CHEB - 1)
    solution = list(direction)
    for iteration in range(CHEB - 1):
        scaled_resid = [1.0 - zero] + [-c for c in solution[:-1]]
        rho_new = 1.0 / (2.0 * sigma - rho_now)
        direction = [
            rho_new * rho_now * d + 2.0 * rho_new / delta * r
            for d, r in zip(direction, scaled_resid)
        ]
        solution = [s + d for s, d in zip(solution, direction)]
        rho_now = rho_new
    return solution


def body(rhs, levels, face_source, subface, orientation, send_list, parent, coarse_inverse):
    tables = gll_tables(NODES)
    weights, stiffness, half_low, half_high = tables
    count = NODES
    elements = rhs.shape[1]
    scale = jnp.exp2(-levels.astype(jnp.float32))
    inv_diag = 1.0 / (diag_pattern(tables)[:, None] * scale[None, :])
    face_mass = weights[:, None] * weights[None, :]

    def operator(fields):
        number = len(fields)
        field = jnp.concatenate(fields, axis=1) if number > 1 else fields[0]
        tiled_scale = jnp.tile(scale, number)
        cube = field.reshape(count, count, count, -1)
        traces = face_traces(cube)
        neighbour = orient_faces(
            neighbour_traces(traces, face_source, send_list, number),
            jnp.tile(orientation, (1, number)),
            jnp.tile(subface, (1, number)),
            half_low,
            half_high,
        )
        jumps = PENALTY * face_mass[None, :, :, None] * (traces - neighbour)
        total = add_faces(cell_term(cube, weights, stiffness), jumps)
        total = total.reshape(count * count * count, -1) * tiled_scale[None, :]
        return [total[:, k * elements:(k + 1) * elements] for k in range(number)]

    def paired_round(iteration, carry):
        power, previous, latest, krylov_stack, image_stack = carry
        both = operator([power, latest])
        latest = inv_diag * both[1]
        return (
            inv_diag * both[0],
            power,
            latest,
            lax.dynamic_update_index_in_dim(krylov_stack, latest, iteration, 0),
            lax.dynamic_update_index_in_dim(image_stack, both[1], iteration, 0),
        )

    start = inv_diag * rhs
    history = jnp.zeros((POWER,) + rhs.shape, rhs.dtype)
    power, previous, latest, krylov_stack, image_stack = lax.fori_loop(
        0, POWER, paired_round, (rhs, rhs, start, history, history)
    )
    krylov = [start] + [krylov_stack[j] for j in range(POWER)]
    images = [image_stack[j] for j in range(POWER)] + [operator([latest])[0]]

    mass = (weights[:, None, None] * weights[None, :, None] * weights[None, None, :]).reshape(
        count * count * count, 1
    )
    cells = coarse_inverse.shape[1]
    element_mass = jnp.stack([jnp.sum(mass * v, axis=0) for v in [rhs] + images], axis=1) / 8.0
    partial = jax.ops.segment_sum(element_mass, parent[0], num_segments=cells)
    norms = jnp.stack([jnp.sum(power * power), jnp.sum(previous * previous)])
    narrow = lax.axis_size("narrow")
    local_block = jnp.concatenate([norms, partial.reshape(-1)])
    shared = jnp.broadcast_to(local_block[None], (narrow,) + local_block.shape)
    block = jnp.sum(lax.all_to_all(shared, "narrow", 0, 0, tiled=True), axis=0)
    wide = lax.axis_size("wide")
    spread = jnp.broadcast_to(block[None, :2], (wide, 2))
    norms = jnp.sum(lax.all_to_all(spread, "wide", 0, 0, tiled=True), axis=0)
    restricted = block[2:].reshape(cells, len(images) + 1)

    estimate = jnp.sqrt(norms[0] / norms[1])
    coefficients = chebyshev_coefficients(estimate)
    solution = coefficients[0] * krylov[0]
    applied = coefficients[0] * images[0]
    coarse_res = restricted[:, 0] - coefficients[0] * restricted[:, 1]
    for j in range(1, CHEB):
        solution = solution + coefficients[j] * krylov[j]
        applied = applied + coefficients[j] * images[j]
        coarse_res = coarse_res - coefficients[j] * restricted[:, j + 1]
    residual = rhs - applied
    coarse_cor = jnp.dot(coarse_inverse[0], coarse_res, precision=HIGHEST)
    corrected = solution + coarse_cor[parent[0]][None, :]
    return (corrected, residual)


def solution(mesh):
    in_specs = (
        P(None, ("wide", "narrow")),
        P(("wide", "narrow")),
        P(None, ("wide", "narrow")),
        P(None, ("wide", "narrow")),
        P(None, ("wide", "narrow")),
        P(("wide", "narrow"), None),
        P("wide", "narrow"),
        P("wide", None, None),
    )
    out_specs = (P(None, ("wide", "narrow")), P(None, ("wide", "narrow")))
    return jax.shard_map(body, mesh=mesh, in_specs=in_specs, out_specs=out_specs, check_vma=False)
```

```python
import jax
import jax.numpy as jnp
import numpy as np
from jax import lax
from jax.sharding import PartitionSpec as P

NODES = 8
POWER = 3
CHEB = 4


PENALTY = 32.0
SAFETY = 1.2
RANGE_RATIO = 8.0
HIGHEST = lax.Precision.HIGHEST


def legendre_rows(points, count):
    rows_list = [points * 0.0 + 1.0, points.copy()]
    for order in range(2, count):
        rows_list.append(
            ((2 * order - 1) * points * rows_list[order - 1] - (order - 1) * rows_list[order - 2])
            / order
        )
    return rows_list


def gll_tables(count):
    degree_top = count - 1
    node_pos = np.cos(np.pi * np.arange(count) / degree_top)
    for newton_step in range(60):
        values_table = legendre_rows(node_pos, count)
        node_pos = node_pos - (
            node_pos * values_table[degree_top] - values_table[degree_top - 1]
        ) / (count * values_table[degree_top])
    node_pos = node_pos[::-1].copy()
    node_pos[0] = -1.0
    node_pos[-1] = 1.0
    values_table = legendre_rows(node_pos, count)
    weights = 2.0 / (degree_top * count * values_table[degree_top] ** 2)
    barycentric = np.array(
        [
            1.0 / np.prod([node_pos[j] - node_pos[k] for k in range(count) if k != j])
            for j in range(count)
        ]
    )
    derivative = np.zeros((count, count))
    for i in range(count):
        for j in range(count):
            if i != j:
                derivative[i, j] = barycentric[j] / barycentric[i] / (node_pos[i] - node_pos[j])
        derivative[i, i] = -np.sum(derivative[i])
    stiffness = derivative.T @ (weights[:, None] * derivative)

    def interpolate(targets):
        matrix = np.ones((count, count))
        for j in range(count):
            for k in range(count):
                if k != j:
                    matrix[:, j] *= (targets - node_pos[k]) / (node_pos[j] - node_pos[k])
        return matrix

    half_low = interpolate((node_pos - 1.0) / 2.0)
    half_high = interpolate((node_pos + 1.0) / 2.0)
    return tuple(
        (
            jnp.asarray(table, dtype=jnp.float32)
            for table in (weights, stiffness, half_low, half_high)
        )
    )


def face_traces(cube):
    return jnp.stack([cube[0], cube[-1], cube[:, 0], cube[:, -1], cube[:, :, 0], cube[:, :, -1]])


def add_faces(cube, values):
    count = cube.shape[0]
    first = (jnp.arange(count) == 0).astype(cube.dtype)
    last = (jnp.arange(count) == count - 1).astype(cube.dtype)
    for index in range(6):
        axis, pick = index // 2, (first, last)[index % 2]
        shape = [1] * cube.ndim
        shape[axis] = count
        cube = cube + pick.reshape(shape) * jnp.expand_dims(values[index], axis)
    return cube


def orient_faces(neighbour, orientation, subface, half_low, half_high):
    bit_one = (orientation % 2)[:, None, None, :] == 1
    bit_two = (orientation // 2 % 2)[:, None, None, :] == 1
    bit_four = (orientation // 4)[:, None, None, :] == 1
    turned = jnp.where(bit_one, neighbour[:, ::-1], neighbour)
    turned = jnp.where(bit_two, turned[:, :, ::-1], turned)
    turned = jnp.where(bit_four, jnp.swapaxes(turned, 1, 2), turned)
    hanging = (subface > 0)[:, None, None, :]
    quad_first = ((subface - 1) % 2)[:, None, None, :] == 0
    quad_second = ((subface - 1) // 2)[:, None, None, :] == 0
    low_first = jnp.einsum("ai,fibe->fabe", half_low, turned, precision=HIGHEST)
    high_first = jnp.einsum("ai,fibe->fabe", half_high, turned, precision=HIGHEST)
    first_pass = jnp.where(quad_first, low_first, high_first)
    low_second = jnp.einsum("bj,faje->fabe", half_low, first_pass, precision=HIGHEST)
    high_second = jnp.einsum("bj,faje->fabe", half_high, first_pass, precision=HIGHEST)
    second_pass = jnp.where(quad_second, low_second, high_second)
    return jnp.where(hanging, second_pass, turned)


def cell_term(cube, weights, stiffness):
    first_axis = jnp.einsum("ai,ijke->ajke", stiffness, cube, precision=HIGHEST) * (
        weights[None, :, None, None] * weights[None, None, :, None]
    )
    second_axis = jnp.einsum("bj,ijke->ibke", stiffness, cube, precision=HIGHEST) * (
        weights[:, None, None, None] * weights[None, None, :, None]
    )
    third_axis = jnp.einsum("ck,ijke->ijce", stiffness, cube, precision=HIGHEST) * (
        weights[:, None, None, None] * weights[None, :, None, None]
    )
    return first_axis + second_axis + third_axis


def diag_pattern(tables):
    weights, stiffness, half_low, half_high = tables
    count = weights.shape[0]
    stiff_diag = jnp.diagonal(stiffness)
    cell_diag = (
        stiff_diag[:, None, None] * weights[None, :, None] * weights[None, None, :]
        + weights[:, None, None] * stiff_diag[None, :, None] * weights[None, None, :]
        + weights[:, None, None] * weights[None, :, None] * stiff_diag[None, None, :]
    )
    face_mass = PENALTY * weights[:, None] * weights[None, :]
    face_values = jnp.broadcast_to(face_mass[None, :, :, None], (6, count, count, 1))
    pattern = add_faces(cell_diag[:, :, :, None], face_values)
    return pattern.reshape(count * count * count)


def neighbour_traces(traces, face_source, send_list, fields, cover):
    count = traces.shape[1]
    elements = traces.shape[3] // fields
    wide = lax.axis_size("wide")
    rows = fields * count * count
    local = (
        traces.reshape(6, count * count, fields, elements)
        .transpose(2, 1, 0, 3)
        .reshape(rows, 6 * elements)
    )
    picked = local[:, send_list[0]]
    outgoing = picked.T.reshape(3, lax.axis_size("narrow"), -1)
    swapped = lax.all_to_all(outgoing, "narrow", split_axis=1, concat_axis=1, tiled=True)
    swapped, cover = lax.optimization_barrier((swapped, cover))
    up = [(i, i + 1) for i in range(wide - 1)]
    down = [(i + 1, i) for i in range(wide - 1)]
    before = lax.ppermute(swapped[2], "wide", up)
    after = lax.ppermute(swapped[0], "wide", down)
    incoming = jnp.stack([before, swapped[1], after])
    received = incoming.reshape(-1, rows).T
    pool = jnp.concatenate([local, received, jnp.zeros((rows, 1), jnp.float32)], axis=1)
    columns = jnp.where(face_source < 0, pool.shape[1] - 1, face_source).reshape(-1)
    gathered = pool[:, columns]
    return (
        gathered.reshape(fields, count * count, 6, elements)
        .transpose(2, 1, 0, 3)
        .reshape(6, count, count, fields * elements)
    ), cover


def chebyshev_coefficients(estimate):
    lam_max = SAFETY * estimate
    lam_min = lam_max / RANGE_RATIO
    theta = (lam_max + lam_min) / 2.0
    delta = (lam_max - lam_min) / 2.0
    sigma = theta / delta
    rho_now = 1.0 / sigma
    zero = jnp.zeros_like(estimate)
    direction = [1.0 / theta] + [zero] * (CHEB - 1)
    solution = list(direction)
    for iteration in range(CHEB - 1):
        scaled_resid = [1.0 - zero] + [-c for c in solution[:-1]]
        rho_new = 1.0 / (2.0 * sigma - rho_now)
        direction = [
            rho_new * rho_now * d + 2.0 * rho_new / delta * r
            for d, r in zip(direction, scaled_resid)
        ]
        solution = [s + d for s, d in zip(solution, direction)]
        rho_now = rho_new
    return solution


def body(rhs, levels, face_source, subface, orientation, send_list, parent, coarse_inverse):
    tables = gll_tables(NODES)
    weights, stiffness, half_low, half_high = tables
    count = NODES
    elements = rhs.shape[1]
    scale = jnp.exp2(-levels.astype(jnp.float32))
    inv_diag = 1.0 / (diag_pattern(tables)[:, None] * scale[None, :])
    face_mass = weights[:, None] * weights[None, :]

    def operator(fields):
        number = len(fields)
        field = jnp.concatenate(fields, axis=1) if number > 1 else fields[0]
        tiled_scale = jnp.tile(scale, number)
        cube = field.reshape(count, count, count, -1)
        traces = face_traces(cube)
        gathered, cell = neighbour_traces(
            traces, face_source, send_list, number, cell_term(cube, weights, stiffness)
        )
        neighbour = orient_faces(
            gathered,
            jnp.tile(orientation, (1, number)),
            jnp.tile(subface, (1, number)),
            half_low,
            half_high,
        )
        jumps = PENALTY * face_mass[None, :, :, None] * (traces - neighbour)
        total = add_faces(cell, jumps)
        total = total.reshape(count * count * count, -1) * tiled_scale[None, :]
        return [total[:, k * elements:(k + 1) * elements] for k in range(number)]

    def paired_round(iteration, carry):
        power, previous, latest, krylov_stack, image_stack = carry
        both = operator([power, latest])
        latest = inv_diag * both[1]
        return (
            inv_diag * both[0],
            power,
            latest,
            lax.dynamic_update_index_in_dim(krylov_stack, latest, iteration, 0),
            lax.dynamic_update_index_in_dim(image_stack, both[1], iteration, 0),
        )

    start = inv_diag * rhs
    history = jnp.zeros((POWER,) + rhs.shape, rhs.dtype)
    power, previous, latest, krylov_stack, image_stack = lax.fori_loop(
        0, POWER, paired_round, (rhs, rhs, start, history, history)
    )
    krylov = [start] + [krylov_stack[j] for j in range(POWER)]
    images = [image_stack[j] for j in range(POWER)] + [operator([latest])[0]]

    mass = (weights[:, None, None] * weights[None, :, None] * weights[None, None, :]).reshape(
        count * count * count, 1
    )
    cells = coarse_inverse.shape[1]
    element_mass = jnp.stack([jnp.sum(mass * v, axis=0) for v in [rhs] + images], axis=1) / 8.0
    partial = jax.ops.segment_sum(element_mass, parent[0], num_segments=cells)
    norms = jnp.stack([jnp.sum(power * power), jnp.sum(previous * previous)])
    narrow = lax.axis_size("narrow")
    local_block = jnp.concatenate([norms, partial.reshape(-1)])
    shared = jnp.broadcast_to(local_block[None], (narrow,) + local_block.shape)
    block = jnp.sum(lax.all_to_all(shared, "narrow", 0, 0, tiled=True), axis=0)
    wide = lax.axis_size("wide")
    spread = jnp.broadcast_to(block[None, :2], (wide, 2))
    norms = jnp.sum(lax.all_to_all(spread, "wide", 0, 0, tiled=True), axis=0)
    restricted = block[2:].reshape(cells, len(images) + 1)

    estimate = jnp.sqrt(norms[0] / norms[1])
    coefficients = chebyshev_coefficients(estimate)
    solution = coefficients[0] * krylov[0]
    applied = coefficients[0] * images[0]
    coarse_res = restricted[:, 0] - coefficients[0] * restricted[:, 1]
    for j in range(1, CHEB):
        solution = solution + coefficients[j] * krylov[j]
        applied = applied + coefficients[j] * images[j]
        coarse_res = coarse_res - coefficients[j] * restricted[:, j + 1]
    residual = rhs - applied
    coarse_cor = jnp.dot(coarse_inverse[0], coarse_res, precision=HIGHEST)
    corrected = solution + coarse_cor[parent[0]][None, :]
    return (corrected, residual)


def solution(mesh):
    in_specs = (
        P(None, ("wide", "narrow")),
        P(("wide", "narrow")),
        P(None, ("wide", "narrow")),
        P(None, ("wide", "narrow")),
        P(None, ("wide", "narrow")),
        P(("wide", "narrow"), None),
        P("wide", "narrow"),
        P("wide", None, None),
    )
    out_specs = (P(None, ("wide", "narrow")), P(None, ("wide", "narrow")))
    return jax.shard_map(body, mesh=mesh, in_specs=in_specs, out_specs=out_specs, check_vma=False)
```

```python
import jax
import jax.numpy as jnp
import numpy as np
from jax import lax
from jax.sharding import PartitionSpec as P

NODES = 8
POWER = 3
CHEB = 4


PENALTY = 32.0
SAFETY = 1.2
RANGE_RATIO = 8.0
HIGHEST = lax.Precision.HIGHEST


def legendre_rows(points, count):
    rows_list = [points * 0.0 + 1.0, points.copy()]
    for order in range(2, count):
        rows_list.append(
            ((2 * order - 1) * points * rows_list[order - 1] - (order - 1) * rows_list[order - 2])
            / order
        )
    return rows_list


def gll_tables(count):
    degree_top = count - 1
    node_pos = np.cos(np.pi * np.arange(count) / degree_top)
    for newton_step in range(60):
        values_table = legendre_rows(node_pos, count)
        node_pos = node_pos - (
            node_pos * values_table[degree_top] - values_table[degree_top - 1]
        ) / (count * values_table[degree_top])
    node_pos = node_pos[::-1].copy()
    node_pos[0] = -1.0
    node_pos[-1] = 1.0
    values_table = legendre_rows(node_pos, count)
    weights = 2.0 / (degree_top * count * values_table[degree_top] ** 2)
    barycentric = np.array(
        [
            1.0 / np.prod([node_pos[j] - node_pos[k] for k in range(count) if k != j])
            for j in range(count)
        ]
    )
    derivative = np.zeros((count, count))
    for i in range(count):
        for j in range(count):
            if i != j:
                derivative[i, j] = barycentric[j] / barycentric[i] / (node_pos[i] - node_pos[j])
        derivative[i, i] = -np.sum(derivative[i])
    stiffness = derivative.T @ (weights[:, None] * derivative)

    def interpolate(targets):
        matrix = np.ones((count, count))
        for j in range(count):
            for k in range(count):
                if k != j:
                    matrix[:, j] *= (targets - node_pos[k]) / (node_pos[j] - node_pos[k])
        return matrix

    half_low = interpolate((node_pos - 1.0) / 2.0)
    half_high = interpolate((node_pos + 1.0) / 2.0)
    return tuple(
        (
            jnp.asarray(table, dtype=jnp.float32)
            for table in (weights, stiffness, half_low, half_high)
        )
    )


def face_traces(cube):
    return jnp.stack([cube[0], cube[-1], cube[:, 0], cube[:, -1], cube[:, :, 0], cube[:, :, -1]])


def add_faces(cube, values):
    count = cube.shape[0]
    first = (jnp.arange(count) == 0).astype(cube.dtype)
    last = (jnp.arange(count) == count - 1).astype(cube.dtype)
    for index in range(6):
        axis, pick = index // 2, (first, last)[index % 2]
        shape = [1] * cube.ndim
        shape[axis] = count
        cube = cube + pick.reshape(shape) * jnp.expand_dims(values[index], axis)
    return cube


def orient_faces(neighbour, orientation, subface, half_low, half_high):
    bit_one = (orientation % 2)[:, None, None, :] == 1
    bit_two = (orientation // 2 % 2)[:, None, None, :] == 1
    bit_four = (orientation // 4)[:, None, None, :] == 1
    turned = jnp.where(bit_one, neighbour[:, ::-1], neighbour)
    turned = jnp.where(bit_two, turned[:, :, ::-1], turned)
    turned = jnp.where(bit_four, jnp.swapaxes(turned, 1, 2), turned)
    hanging = (subface > 0)[:, None, None, :]
    quad_first = ((subface - 1) % 2)[:, None, None, :] == 0
    quad_second = ((subface - 1) // 2)[:, None, None, :] == 0
    low_first = jnp.einsum("ai,fibe->fabe", half_low, turned, precision=HIGHEST)
    high_first = jnp.einsum("ai,fibe->fabe", half_high, turned, precision=HIGHEST)
    first_pass = jnp.where(quad_first, low_first, high_first)
    low_second = jnp.einsum("bj,faje->fabe", half_low, first_pass, precision=HIGHEST)
    high_second = jnp.einsum("bj,faje->fabe", half_high, first_pass, precision=HIGHEST)
    second_pass = jnp.where(quad_second, low_second, high_second)
    return jnp.where(hanging, second_pass, turned)


def cell_term(cube, weights, stiffness):
    first_axis = jnp.einsum("ai,ijke->ajke", stiffness, cube, precision=HIGHEST) * (
        weights[None, :, None, None] * weights[None, None, :, None]
    )
    second_axis = jnp.einsum("bj,ijke->ibke", stiffness, cube, precision=HIGHEST) * (
        weights[:, None, None, None] * weights[None, None, :, None]
    )
    third_axis = jnp.einsum("ck,ijke->ijce", stiffness, cube, precision=HIGHEST) * (
        weights[:, None, None, None] * weights[None, :, None, None]
    )
    return first_axis + second_axis + third_axis


def diag_pattern(tables):
    weights, stiffness, half_low, half_high = tables
    count = weights.shape[0]
    stiff_diag = jnp.diagonal(stiffness)
    cell_diag = (
        stiff_diag[:, None, None] * weights[None, :, None] * weights[None, None, :]
        + weights[:, None, None] * stiff_diag[None, :, None] * weights[None, None, :]
        + weights[:, None, None] * weights[None, :, None] * stiff_diag[None, None, :]
    )
    face_mass = PENALTY * weights[:, None] * weights[None, :]
    face_values = jnp.broadcast_to(face_mass[None, :, :, None], (6, count, count, 1))
    pattern = add_faces(cell_diag[:, :, :, None], face_values)
    return pattern.reshape(count * count * count)


def neighbour_traces(traces, face_source, send_list, fields, cover):
    count = traces.shape[1]
    elements = traces.shape[3] // fields
    wide = lax.axis_size("wide")
    rows = fields * count * count
    local = (
        traces.reshape(6, count * count, fields, elements)
        .transpose(2, 1, 0, 3)
        .reshape(rows, 6 * elements)
    )
    picked = local[:, send_list[0]]
    outgoing = picked.T.reshape(3, lax.axis_size("narrow"), -1)
    swapped = lax.all_to_all(outgoing, "narrow", split_axis=1, concat_axis=1, tiled=True)
    if fields > 1:
        swapped, cover = lax.optimization_barrier((swapped, cover))
    up = [(i, i + 1) for i in range(wide - 1)]
    down = [(i + 1, i) for i in range(wide - 1)]
    before = lax.ppermute(swapped[2], "wide", up)
    after = lax.ppermute(swapped[0], "wide", down)
    incoming = jnp.stack([before, swapped[1], after])
    received = incoming.reshape(-1, rows).T
    pool = jnp.concatenate([local, received, jnp.zeros((rows, 1), jnp.float32)], axis=1)
    columns = jnp.where(face_source < 0, pool.shape[1] - 1, face_source).reshape(-1)
    gathered = pool[:, columns]
    return (
        gathered.reshape(fields, count * count, 6, elements)
        .transpose(2, 1, 0, 3)
        .reshape(6, count, count, fields * elements)
    ), cover


def chebyshev_coefficients(estimate):
    lam_max = SAFETY * estimate
    lam_min = lam_max / RANGE_RATIO
    theta = (lam_max + lam_min) / 2.0
    delta = (lam_max - lam_min) / 2.0
    sigma = theta / delta
    rho_now = 1.0 / sigma
    zero = jnp.zeros_like(estimate)
    direction = [1.0 / theta] + [zero] * (CHEB - 1)
    solution = list(direction)
    for iteration in range(CHEB - 1):
        scaled_resid = [1.0 - zero] + [-c for c in solution[:-1]]
        rho_new = 1.0 / (2.0 * sigma - rho_now)
        direction = [
            rho_new * rho_now * d + 2.0 * rho_new / delta * r
            for d, r in zip(direction, scaled_resid)
        ]
        solution = [s + d for s, d in zip(solution, direction)]
        rho_now = rho_new
    return solution


def body(rhs, levels, face_source, subface, orientation, send_list, parent, coarse_inverse):
    tables = gll_tables(NODES)
    weights, stiffness, half_low, half_high = tables
    count = NODES
    elements = rhs.shape[1]
    scale = jnp.exp2(-levels.astype(jnp.float32))
    inv_diag = 1.0 / (diag_pattern(tables)[:, None] * scale[None, :])
    face_mass = weights[:, None] * weights[None, :]

    def operator(fields):
        number = len(fields)
        field = jnp.concatenate(fields, axis=1) if number > 1 else fields[0]
        tiled_scale = jnp.tile(scale, number)
        cube = field.reshape(count, count, count, -1)
        traces = face_traces(cube)
        gathered, cell = neighbour_traces(
            traces, face_source, send_list, number, cell_term(cube, weights, stiffness)
        )
        neighbour = orient_faces(
            gathered,
            jnp.tile(orientation, (1, number)),
            jnp.tile(subface, (1, number)),
            half_low,
            half_high,
        )
        jumps = PENALTY * face_mass[None, :, :, None] * (traces - neighbour)
        total = add_faces(cell, jumps)
        total = total.reshape(count * count * count, -1) * tiled_scale[None, :]
        return [total[:, k * elements:(k + 1) * elements] for k in range(number)]

    def paired_round(iteration, carry):
        power, previous, latest, krylov_stack, image_stack = carry
        both = operator([power, latest])
        latest = inv_diag * both[1]
        return (
            inv_diag * both[0],
            power,
            latest,
            lax.dynamic_update_index_in_dim(krylov_stack, latest, iteration, 0),
            lax.dynamic_update_index_in_dim(image_stack, both[1], iteration, 0),
        )

    start = inv_diag * rhs
    history = jnp.zeros((POWER,) + rhs.shape, rhs.dtype)
    power, previous, latest, krylov_stack, image_stack = lax.fori_loop(
        0, POWER, paired_round, (rhs, rhs, start, history, history)
    )
    krylov = [start] + [krylov_stack[j] for j in range(POWER)]
    images = [image_stack[j] for j in range(POWER)] + [operator([latest])[0]]

    mass = (weights[:, None, None] * weights[None, :, None] * weights[None, None, :]).reshape(
        count * count * count, 1
    )
    cells = coarse_inverse.shape[1]
    element_mass = jnp.stack([jnp.sum(mass * v, axis=0) for v in [rhs] + images], axis=1) / 8.0
    partial = jax.ops.segment_sum(element_mass, parent[0], num_segments=cells)
    norms = jnp.stack([jnp.sum(power * power), jnp.sum(previous * previous)])
    narrow = lax.axis_size("narrow")
    local_block = jnp.concatenate([norms, partial.reshape(-1)])
    shared = jnp.broadcast_to(local_block[None], (narrow,) + local_block.shape)
    block = jnp.sum(lax.all_to_all(shared, "narrow", 0, 0, tiled=True), axis=0)
    wide = lax.axis_size("wide")
    spread = jnp.broadcast_to(block[None, :2], (wide, 2))
    norms = jnp.sum(lax.all_to_all(spread, "wide", 0, 0, tiled=True), axis=0)
    restricted = block[2:].reshape(cells, len(images) + 1)

    estimate = jnp.sqrt(norms[0] / norms[1])
    coefficients = chebyshev_coefficients(estimate)
    solution = coefficients[0] * krylov[0]
    applied = coefficients[0] * images[0]
    coarse_res = restricted[:, 0] - coefficients[0] * restricted[:, 1]
    for j in range(1, CHEB):
        solution = solution + coefficients[j] * krylov[j]
        applied = applied + coefficients[j] * images[j]
        coarse_res = coarse_res - coefficients[j] * restricted[:, j + 1]
    residual = rhs - applied
    coarse_cor = jnp.dot(coarse_inverse[0], coarse_res, precision=HIGHEST)
    corrected = solution + coarse_cor[parent[0]][None, :]
    return (corrected, residual)


def solution(mesh):
    in_specs = (
        P(None, ("wide", "narrow")),
        P(("wide", "narrow")),
        P(None, ("wide", "narrow")),
        P(None, ("wide", "narrow")),
        P(None, ("wide", "narrow")),
        P(("wide", "narrow"), None),
        P("wide", "narrow"),
        P("wide", None, None),
    )
    out_specs = (P(None, ("wide", "narrow")), P(None, ("wide", "narrow")))
    return jax.shard_map(body, mesh=mesh, in_specs=in_specs, out_specs=out_specs, check_vma=False)
```

```python
import jax
import jax.numpy as jnp
import numpy as np
from jax import lax
from jax.sharding import PartitionSpec as P

NODES = 8
POWER = 3
CHEB = 4


PENALTY = 32.0
SAFETY = 1.2
RANGE_RATIO = 8.0
HIGHEST = lax.Precision.HIGHEST


def legendre_rows(points, count):
    rows_list = [points * 0.0 + 1.0, points.copy()]
    for order in range(2, count):
        rows_list.append(
            ((2 * order - 1) * points * rows_list[order - 1] - (order - 1) * rows_list[order - 2])
            / order
        )
    return rows_list


def gll_tables(count):
    degree_top = count - 1
    node_pos = np.cos(np.pi * np.arange(count) / degree_top)
    for newton_step in range(60):
        values_table = legendre_rows(node_pos, count)
        node_pos = node_pos - (
            node_pos * values_table[degree_top] - values_table[degree_top - 1]
        ) / (count * values_table[degree_top])
    node_pos = node_pos[::-1].copy()
    node_pos[0] = -1.0
    node_pos[-1] = 1.0
    values_table = legendre_rows(node_pos, count)
    weights = 2.0 / (degree_top * count * values_table[degree_top] ** 2)
    barycentric = np.array(
        [
            1.0 / np.prod([node_pos[j] - node_pos[k] for k in range(count) if k != j])
            for j in range(count)
        ]
    )
    derivative = np.zeros((count, count))
    for i in range(count):
        for j in range(count):
            if i != j:
                derivative[i, j] = barycentric[j] / barycentric[i] / (node_pos[i] - node_pos[j])
        derivative[i, i] = -np.sum(derivative[i])
    stiffness = derivative.T @ (weights[:, None] * derivative)

    def interpolate(targets):
        matrix = np.ones((count, count))
        for j in range(count):
            for k in range(count):
                if k != j:
                    matrix[:, j] *= (targets - node_pos[k]) / (node_pos[j] - node_pos[k])
        return matrix

    half_low = interpolate((node_pos - 1.0) / 2.0)
    half_high = interpolate((node_pos + 1.0) / 2.0)
    return tuple(
        (
            jnp.asarray(table, dtype=jnp.float32)
            for table in (weights, stiffness, half_low, half_high)
        )
    )


def face_traces(cube):
    return jnp.stack([cube[0], cube[-1], cube[:, 0], cube[:, -1], cube[:, :, 0], cube[:, :, -1]])


def add_faces(cube, values):
    count = cube.shape[0]
    first = (jnp.arange(count) == 0).astype(cube.dtype)
    last = (jnp.arange(count) == count - 1).astype(cube.dtype)
    for index in range(6):
        axis, pick = index // 2, (first, last)[index % 2]
        shape = [1] * cube.ndim
        shape[axis] = count
        cube = cube + pick.reshape(shape) * jnp.expand_dims(values[index], axis)
    return cube


def orient_masks(orientation, subface):
    bit_one = (orientation % 2)[:, None, None, :] == 1
    bit_two = (orientation // 2 % 2)[:, None, None, :] == 1
    bit_four = (orientation // 4)[:, None, None, :] == 1
    hanging = (subface > 0)[:, None, None, :]
    quad_first = ((subface - 1) % 2)[:, None, None, :] == 0
    quad_second = ((subface - 1) // 2)[:, None, None, :] == 0
    return bit_one, bit_two, bit_four, hanging, quad_first, quad_second


def orient_faces(neighbour, masks, half_low, half_high):
    bit_one, bit_two, bit_four, hanging, quad_first, quad_second = masks
    turned = jnp.where(bit_one, neighbour[:, ::-1], neighbour)
    turned = jnp.where(bit_two, turned[:, :, ::-1], turned)
    turned = jnp.where(bit_four, jnp.swapaxes(turned, 1, 2), turned)
    low_first = jnp.einsum("ai,fibe->fabe", half_low, turned, precision=HIGHEST)
    high_first = jnp.einsum("ai,fibe->fabe", half_high, turned, precision=HIGHEST)
    first_pass = jnp.where(quad_first, low_first, high_first)
    low_second = jnp.einsum("bj,faje->fabe", half_low, first_pass, precision=HIGHEST)
    high_second = jnp.einsum("bj,faje->fabe", half_high, first_pass, precision=HIGHEST)
    second_pass = jnp.where(quad_second, low_second, high_second)
    return jnp.where(hanging, second_pass, turned)


def cell_term(cube, weights, stiffness):
    first_axis = jnp.einsum("ai,ijke->ajke", stiffness, cube, precision=HIGHEST) * (
        weights[None, :, None, None] * weights[None, None, :, None]
    )
    second_axis = jnp.einsum("bj,ijke->ibke", stiffness, cube, precision=HIGHEST) * (
        weights[:, None, None, None] * weights[None, None, :, None]
    )
    third_axis = jnp.einsum("ck,ijke->ijce", stiffness, cube, precision=HIGHEST) * (
        weights[:, None, None, None] * weights[None, :, None, None]
    )
    return first_axis + second_axis + third_axis


def diag_pattern(tables):
    weights, stiffness, half_low, half_high = tables
    count = weights.shape[0]
    stiff_diag = jnp.diagonal(stiffness)
    cell_diag = (
        stiff_diag[:, None, None] * weights[None, :, None] * weights[None, None, :]
        + weights[:, None, None] * stiff_diag[None, :, None] * weights[None, None, :]
        + weights[:, None, None] * weights[None, :, None] * stiff_diag[None, None, :]
    )
    face_mass = PENALTY * weights[:, None] * weights[None, :]
    face_values = jnp.broadcast_to(face_mass[None, :, :, None], (6, count, count, 1))
    pattern = add_faces(cell_diag[:, :, :, None], face_values)
    return pattern.reshape(count * count * count)


def neighbour_traces(traces, face_source, send_list, fields):
    count = traces.shape[1]
    elements = traces.shape[3] // fields
    wide = lax.axis_size("wide")
    rows = fields * count * count
    local = (
        traces.reshape(6, count * count, fields, elements)
        .transpose(2, 1, 0, 3)
        .reshape(rows, 6 * elements)
    )
    picked = local[:, send_list[0]]
    outgoing = picked.T.reshape(3, lax.axis_size("narrow"), -1)
    swapped = lax.all_to_all(outgoing, "narrow", split_axis=1, concat_axis=1, tiled=True)
    up = [(i, i + 1) for i in range(wide - 1)]
    down = [(i + 1, i) for i in range(wide - 1)]
    before = lax.ppermute(swapped[2], "wide", up)
    after = lax.ppermute(swapped[0], "wide", down)
    incoming = jnp.stack([before, swapped[1], after])
    received = incoming.reshape(-1, rows).T
    pool = jnp.concatenate([local, received, jnp.zeros((rows, 1), jnp.float32)], axis=1)
    columns = jnp.where(face_source < 0, pool.shape[1] - 1, face_source).reshape(-1)
    gathered = pool[:, columns]
    return (
        gathered.reshape(fields, count * count, 6, elements)
        .transpose(2, 1, 0, 3)
        .reshape(6, count, count, fields * elements)
    )


def chebyshev_coefficients(estimate):
    lam_max = SAFETY * estimate
    lam_min = lam_max / RANGE_RATIO
    theta = (lam_max + lam_min) / 2.0
    delta = (lam_max - lam_min) / 2.0
    sigma = theta / delta
    rho_now = 1.0 / sigma
    zero = jnp.zeros_like(estimate)
    direction = [1.0 / theta] + [zero] * (CHEB - 1)
    solution = list(direction)
    for iteration in range(CHEB - 1):
        scaled_resid = [1.0 - zero] + [-c for c in solution[:-1]]
        rho_new = 1.0 / (2.0 * sigma - rho_now)
        direction = [
            rho_new * rho_now * d + 2.0 * rho_new / delta * r
            for d, r in zip(direction, scaled_resid)
        ]
        solution = [s + d for s, d in zip(solution, direction)]
        rho_now = rho_new
    return solution


def body(rhs, levels, face_source, subface, orientation, send_list, parent, coarse_inverse):
    tables = gll_tables(NODES)
    weights, stiffness, half_low, half_high = tables
    count = NODES
    elements = rhs.shape[1]
    scale = jnp.exp2(-levels.astype(jnp.float32))
    inv_diag = 1.0 / (diag_pattern(tables)[:, None] * scale[None, :])
    face_mass = weights[:, None] * weights[None, :]

    masks = {
        number: orient_masks(jnp.tile(orientation, (1, number)), jnp.tile(subface, (1, number)))
        for number in (1, 2)
    }

    def operator(fields):
        number = len(fields)
        field = jnp.concatenate(fields, axis=1) if number > 1 else fields[0]
        tiled_scale = jnp.tile(scale, number)
        cube = field.reshape(count, count, count, -1)
        traces = face_traces(cube)
        neighbour = orient_faces(
            neighbour_traces(traces, face_source, send_list, number),
            masks[number],
            half_low,
            half_high,
        )
        jumps = PENALTY * face_mass[None, :, :, None] * (traces - neighbour)
        total = add_faces(cell_term(cube, weights, stiffness), jumps)
        total = total.reshape(count * count * count, -1) * tiled_scale[None, :]
        return [total[:, k * elements:(k + 1) * elements] for k in range(number)]

    def paired_round(iteration, carry):
        power, previous, latest, krylov_stack, image_stack = carry
        both = operator([power, latest])
        latest = inv_diag * both[1]
        return (
            inv_diag * both[0],
            power,
            latest,
            lax.dynamic_update_index_in_dim(krylov_stack, latest, iteration, 0),
            lax.dynamic_update_index_in_dim(image_stack, both[1], iteration, 0),
        )

    start = inv_diag * rhs
    history = jnp.zeros((POWER,) + rhs.shape, rhs.dtype)
    power, previous, latest, krylov_stack, image_stack = lax.fori_loop(
        0, POWER, paired_round, (rhs, rhs, start, history, history)
    )
    krylov = [start] + [krylov_stack[j] for j in range(POWER)]
    images = [image_stack[j] for j in range(POWER)] + [operator([latest])[0]]

    mass = (weights[:, None, None] * weights[None, :, None] * weights[None, None, :]).reshape(
        count * count * count, 1
    )
    cells = coarse_inverse.shape[1]
    element_mass = jnp.stack([jnp.sum(mass * v, axis=0) for v in [rhs] + images], axis=1) / 8.0
    partial = jax.ops.segment_sum(element_mass, parent[0], num_segments=cells)
    norms = jnp.stack([jnp.sum(power * power), jnp.sum(previous * previous)])
    narrow = lax.axis_size("narrow")
    local_block = jnp.concatenate([norms, partial.reshape(-1)])
    shared = jnp.broadcast_to(local_block[None], (narrow,) + local_block.shape)
    block = jnp.sum(lax.all_to_all(shared, "narrow", 0, 0, tiled=True), axis=0)
    wide = lax.axis_size("wide")
    spread = jnp.broadcast_to(block[None, :2], (wide, 2))
    norms = jnp.sum(lax.all_to_all(spread, "wide", 0, 0, tiled=True), axis=0)
    restricted = block[2:].reshape(cells, len(images) + 1)

    estimate = jnp.sqrt(norms[0] / norms[1])
    coefficients = chebyshev_coefficients(estimate)
    solution = coefficients[0] * krylov[0]
    applied = coefficients[0] * images[0]
    coarse_res = restricted[:, 0] - coefficients[0] * restricted[:, 1]
    for j in range(1, CHEB):
        solution = solution + coefficients[j] * krylov[j]
        applied = applied + coefficients[j] * images[j]
        coarse_res = coarse_res - coefficients[j] * restricted[:, j + 1]
    residual = rhs - applied
    coarse_cor = jnp.dot(coarse_inverse[0], coarse_res, precision=HIGHEST)
    corrected = solution + coarse_cor[parent[0]][None, :]
    return (corrected, residual)


def solution(mesh):
    in_specs = (
        P(None, ("wide", "narrow")),
        P(("wide", "narrow")),
        P(None, ("wide", "narrow")),
        P(None, ("wide", "narrow")),
        P(None, ("wide", "narrow")),
        P(("wide", "narrow"), None),
        P("wide", "narrow"),
        P("wide", None, None),
    )
    out_specs = (P(None, ("wide", "narrow")), P(None, ("wide", "narrow")))
    return jax.shard_map(body, mesh=mesh, in_specs=in_specs, out_specs=out_specs, check_vma=False)
```

```python
import jax
import jax.numpy as jnp
import numpy as np
from jax import lax
from jax.sharding import PartitionSpec as P

NODES = 8
POWER = 3
CHEB = 4


PENALTY = 32.0
SAFETY = 1.2
RANGE_RATIO = 8.0
HIGHEST = lax.Precision.HIGHEST


def legendre_rows(points, count):
    rows_list = [points * 0.0 + 1.0, points.copy()]
    for order in range(2, count):
        rows_list.append(
            ((2 * order - 1) * points * rows_list[order - 1] - (order - 1) * rows_list[order - 2])
            / order
        )
    return rows_list


def gll_tables(count):
    degree_top = count - 1
    node_pos = np.cos(np.pi * np.arange(count) / degree_top)
    for newton_step in range(60):
        values_table = legendre_rows(node_pos, count)
        node_pos = node_pos - (
            node_pos * values_table[degree_top] - values_table[degree_top - 1]
        ) / (count * values_table[degree_top])
    node_pos = node_pos[::-1].copy()
    node_pos[0] = -1.0
    node_pos[-1] = 1.0
    values_table = legendre_rows(node_pos, count)
    weights = 2.0 / (degree_top * count * values_table[degree_top] ** 2)
    barycentric = np.array(
        [
            1.0 / np.prod([node_pos[j] - node_pos[k] for k in range(count) if k != j])
            for j in range(count)
        ]
    )
    derivative = np.zeros((count, count))
    for i in range(count):
        for j in range(count):
            if i != j:
                derivative[i, j] = barycentric[j] / barycentric[i] / (node_pos[i] - node_pos[j])
        derivative[i, i] = -np.sum(derivative[i])
    stiffness = derivative.T @ (weights[:, None] * derivative)

    def interpolate(targets):
        matrix = np.ones((count, count))
        for j in range(count):
            for k in range(count):
                if k != j:
                    matrix[:, j] *= (targets - node_pos[k]) / (node_pos[j] - node_pos[k])
        return matrix

    half_low = interpolate((node_pos - 1.0) / 2.0)
    half_high = interpolate((node_pos + 1.0) / 2.0)
    return tuple(
        (
            jnp.asarray(table, dtype=jnp.float32)
            for table in (weights, stiffness, half_low, half_high)
        )
    )


def face_traces(cube):
    return jnp.stack([cube[0], cube[-1], cube[:, 0], cube[:, -1], cube[:, :, 0], cube[:, :, -1]])


def add_faces(cube, values):
    count = cube.shape[0]
    first = (jnp.arange(count) == 0).astype(cube.dtype)
    last = (jnp.arange(count) == count - 1).astype(cube.dtype)
    for index in range(6):
        axis, pick = index // 2, (first, last)[index % 2]
        shape = [1] * cube.ndim
        shape[axis] = count
        cube = cube + pick.reshape(shape) * jnp.expand_dims(values[index], axis)
    return cube


def orient_faces(neighbour, orientation, subface, half_low, half_high):
    bit_one = (orientation % 2)[:, None, None, :] == 1
    bit_two = (orientation // 2 % 2)[:, None, None, :] == 1
    bit_four = (orientation // 4)[:, None, None, :] == 1
    turned = jnp.where(bit_one, neighbour[:, ::-1], neighbour)
    turned = jnp.where(bit_two, turned[:, :, ::-1], turned)
    turned = jnp.where(bit_four, jnp.swapaxes(turned, 1, 2), turned)
    hanging = (subface > 0)[:, None, None, :]
    quad_first = ((subface - 1) % 2)[:, None, None, :] == 0
    quad_second = ((subface - 1) // 2)[:, None, None, :] == 0
    low_first = jnp.einsum("ai,fibe->fabe", half_low, turned, precision=HIGHEST)
    high_first = jnp.einsum("ai,fibe->fabe", half_high, turned, precision=HIGHEST)
    first_pass = jnp.where(quad_first, low_first, high_first)
    low_second = jnp.einsum("bj,faje->fabe", half_low, first_pass, precision=HIGHEST)
    high_second = jnp.einsum("bj,faje->fabe", half_high, first_pass, precision=HIGHEST)
    second_pass = jnp.where(quad_second, low_second, high_second)
    return jnp.where(hanging, second_pass, turned)


def cell_term(cube, weights, stiffness):
    first_axis = jnp.einsum("ai,ijke->ajke", stiffness, cube, precision=HIGHEST) * (
        weights[None, :, None, None] * weights[None, None, :, None]
    )
    second_axis = jnp.einsum("bj,ijke->ibke", stiffness, cube, precision=HIGHEST) * (
        weights[:, None, None, None] * weights[None, None, :, None]
    )
    third_axis = jnp.einsum("ck,ijke->ijce", stiffness, cube, precision=HIGHEST) * (
        weights[:, None, None, None] * weights[None, :, None, None]
    )
    return first_axis + second_axis + third_axis


def diag_pattern(tables):
    weights, stiffness, half_low, half_high = tables
    count = weights.shape[0]
    stiff_diag = jnp.diagonal(stiffness)
    cell_diag = (
        stiff_diag[:, None, None] * weights[None, :, None] * weights[None, None, :]
        + weights[:, None, None] * stiff_diag[None, :, None] * weights[None, None, :]
        + weights[:, None, None] * weights[None, :, None] * stiff_diag[None, None, :]
    )
    face_mass = PENALTY * weights[:, None] * weights[None, :]
    face_values = jnp.broadcast_to(face_mass[None, :, :, None], (6, count, count, 1))
    pattern = add_faces(cell_diag[:, :, :, None], face_values)
    return pattern.reshape(count * count * count)


def neighbour_traces(traces, face_source, send_list, fields):
    count = traces.shape[1]
    elements = traces.shape[3] // fields
    wide = lax.axis_size("wide")
    rows = fields * count * count
    local = (
        traces.reshape(6, count * count, fields, elements)
        .transpose(2, 1, 0, 3)
        .reshape(rows, 6 * elements)
    )
    picked = local[:, send_list[0]]
    outgoing = picked.T.reshape(3, lax.axis_size("narrow"), -1)
    swapped = lax.all_to_all(outgoing, "narrow", split_axis=1, concat_axis=1, tiled=True)
    up = [(i, i + 1) for i in range(wide - 1)]
    down = [(i + 1, i) for i in range(wide - 1)]
    before = lax.ppermute(swapped[2], "wide", up)
    after = lax.ppermute(swapped[0], "wide", down)
    incoming = jnp.stack([before, swapped[1], after])
    received = incoming.reshape(-1, rows).T
    pool = jnp.concatenate([local, received, jnp.zeros((rows, 1), jnp.float32)], axis=1)
    columns = jnp.where(face_source < 0, pool.shape[1] - 1, face_source).reshape(-1)
    gathered = pool[:, columns]
    return (
        gathered.reshape(fields, count * count, 6, elements)
        .transpose(2, 1, 0, 3)
        .reshape(6, count, count, fields * elements)
    )


def chebyshev_coefficients(estimate):
    lam_max = SAFETY * estimate
    lam_min = lam_max / RANGE_RATIO
    theta = (lam_max + lam_min) / 2.0
    delta = (lam_max - lam_min) / 2.0
    sigma = theta / delta
    rho_now = 1.0 / sigma
    zero = jnp.zeros_like(estimate)
    direction = [1.0 / theta] + [zero] * (CHEB - 1)
    solution = list(direction)
    for iteration in range(CHEB - 1):
        scaled_resid = [1.0 - zero] + [-c for c in solution[:-1]]
        rho_new = 1.0 / (2.0 * sigma - rho_now)
        direction = [
            rho_new * rho_now * d + 2.0 * rho_new / delta * r
            for d, r in zip(direction, scaled_resid)
        ]
        solution = [s + d for s, d in zip(solution, direction)]
        rho_now = rho_new
    return solution


def body(rhs, levels, face_source, subface, orientation, send_list, parent, coarse_inverse):
    tables = gll_tables(NODES)
    weights, stiffness, half_low, half_high = tables
    count = NODES
    elements = rhs.shape[1]
    scale = jnp.exp2(-levels.astype(jnp.float32))
    inv_diag = 1.0 / (diag_pattern(tables)[:, None] * scale[None, :])
    face_mass = weights[:, None] * weights[None, :]

    def operator(fields):
        number = len(fields)
        field = jnp.concatenate(fields, axis=1) if number > 1 else fields[0]
        tiled_scale = jnp.tile(scale, number)
        cube = field.reshape(count, count, count, -1)
        traces = face_traces(cube)
        neighbour = orient_faces(
            neighbour_traces(traces, face_source, send_list, number),
            jnp.tile(orientation, (1, number)),
            jnp.tile(subface, (1, number)),
            half_low,
            half_high,
        )
        jumps = PENALTY * face_mass[None, :, :, None] * (traces - neighbour)
        total = add_faces(cell_term(cube, weights, stiffness), jumps)
        total = total.reshape(count * count * count, -1) * tiled_scale[None, :]
        return [total[:, k * elements:(k + 1) * elements] for k in range(number)]

    def paired_round(iteration, carry):
        power, latest, norm_stack, krylov_stack, image_stack = carry
        both = operator([power, latest])
        power = inv_diag * both[0]
        latest = inv_diag * both[1]
        return (
            power,
            latest,
            lax.dynamic_update_index_in_dim(norm_stack, jnp.sum(power * power), iteration, 0),
            lax.dynamic_update_index_in_dim(krylov_stack, latest, iteration, 0),
            lax.dynamic_update_index_in_dim(image_stack, both[1], iteration, 0),
        )

    rounds = max(POWER, CHEB)
    start = inv_diag * rhs
    history = jnp.zeros((rounds,) + rhs.shape, rhs.dtype)
    power, latest, norm_stack, krylov_stack, image_stack = lax.fori_loop(
        0, rounds, paired_round, (rhs, start, jnp.zeros((rounds,), rhs.dtype), history, history)
    )
    krylov = [start] + [krylov_stack[j] for j in range(CHEB - 1)]
    images = [image_stack[j] for j in range(CHEB)]

    mass = (weights[:, None, None] * weights[None, :, None] * weights[None, None, :]).reshape(
        count * count * count, 1
    )
    cells = coarse_inverse.shape[1]
    element_mass = jnp.stack([jnp.sum(mass * v, axis=0) for v in [rhs] + images], axis=1) / 8.0
    partial = jax.ops.segment_sum(element_mass, parent[0], num_segments=cells)
    norms = jnp.stack([norm_stack[POWER - 1], norm_stack[POWER - 2]])
    narrow = lax.axis_size("narrow")
    local_block = jnp.concatenate([norms, partial.reshape(-1)])
    shared = jnp.broadcast_to(local_block[None], (narrow,) + local_block.shape)
    block = jnp.sum(lax.all_to_all(shared, "narrow", 0, 0, tiled=True), axis=0)
    wide = lax.axis_size("wide")
    spread = jnp.broadcast_to(block[None, :2], (wide, 2))
    norms = jnp.sum(lax.all_to_all(spread, "wide", 0, 0, tiled=True), axis=0)
    restricted = block[2:].reshape(cells, len(images) + 1)

    estimate = jnp.sqrt(norms[0] / norms[1])
    coefficients = chebyshev_coefficients(estimate)
    solution = coefficients[0] * krylov[0]
    applied = coefficients[0] * images[0]
    coarse_res = restricted[:, 0] - coefficients[0] * restricted[:, 1]
    for j in range(1, CHEB):
        solution = solution + coefficients[j] * krylov[j]
        applied = applied + coefficients[j] * images[j]
        coarse_res = coarse_res - coefficients[j] * restricted[:, j + 1]
    residual = rhs - applied
    coarse_cor = jnp.dot(coarse_inverse[0], coarse_res, precision=HIGHEST)
    corrected = solution + coarse_cor[parent[0]][None, :]
    return (corrected, residual)


def solution(mesh):
    in_specs = (
        P(None, ("wide", "narrow")),
        P(("wide", "narrow")),
        P(None, ("wide", "narrow")),
        P(None, ("wide", "narrow")),
        P(None, ("wide", "narrow")),
        P(("wide", "narrow"), None),
        P("wide", "narrow"),
        P("wide", None, None),
    )
    out_specs = (P(None, ("wide", "narrow")), P(None, ("wide", "narrow")))
    return jax.shard_map(body, mesh=mesh, in_specs=in_specs, out_specs=out_specs, check_vma=False)
```
